32 devices in a mesh: req: 4 (over z), seq: 2 (over x), tp: 4 (over y, core).
Axes of the slice: x: 2, y: 2, z: 4, core: 2. Of those that a mesh axis runs over, the one named last changes fastest.
Arguments:
- tokens: bfloat16 [8, 256, 2048], P('req', 'seq'), may hold values from -6 to 6
- w_query: bfloat16 [2048, 2048], P(('req', 'seq'), 'tp'), may hold values from -0.125 to 0.125
- w_key: bfloat16 [2048, 2048], P(('req', 'seq'), 'tp'), may hold values from -0.125 to 0.125
- w_value: bfloat16 [2048, 2048], P(('req', 'seq'), 'tp'), may hold values from -0.125 to 0.125
- q_gain: float32 [2048], P('tp'), may hold values from 1 to 4
- k_gain: float32 [2048], P('tp'), may hold values from 1 to 4
- cache_keys: bfloat16 [8, 4096, 2048], P('req', 'seq', 'tp'), may hold values from -140 to 140
- cache_values: bfloat16 [8, 4096, 2048], P('req', 'seq', 'tp'), may hold values from -6 to 6
- sink_keys: bfloat16 [8, 4, 2048], P('req', None, 'tp'), may hold values from -16 to 16
- sink_values: bfloat16 [8, 4, 2048], P('req', None, 'tp'), may hold values from -6 to 6
- sink_pos: int32 [8, 4], P('req'), may hold values from 0 to 8191
- cache_len: int32 [8], P('req'), may hold values from 0 to 32768
- span_len: int32 [8], P('req'), may hold values from 1 to 256, as said below
- window_len: int32 [8], P('req'), may hold values from 2048 to 4096, as said below
Outputs:
- attended: bfloat16 [8, 256, 2048], P('req', 'seq', 'tp')
The draws below stay inside these ranges and needn't reach their ends.
Inputs may be any that keep to these rules, and one draw needn't show every extreme that they name: `span_len`: some request's span has exactly 256 live tokens. `window_len`: some request's window is exactly 4096.
All inputs are finite; a program needn't handle non-finite values.
Results may differ from the reference program's by a relative error of at most 0.022.
Values may be sent and summed in bfloat16 or wider, within the bound.
No kernel may reach another device: no remote copies, remote signals or barrier semaphores. Data moves between devices by JAX's collectives and lax.ppermute only.
A program may use at most 128 MiB of HBM per device.

```python
import math
import jax
import jax.numpy as jnp
from jax import lax

D = 2048
HEADS = 16
HEAD_DIM = 128
WINDOW = 4096
SINKS = 4
REQUESTS = 8
SPAN = 256


def draw_span_len(key, part):
    counts = jax.random.randint(jax.random.fold_in(key, 11), (REQUESTS,), 1, SPAN + 1)
    chosen = jax.random.randint(jax.random.fold_in(key, 12), (), 0, REQUESTS)
    return jnp.where(jnp.arange(REQUESTS) == chosen, SPAN, counts).astype(jnp.int32)


def draw_window_len(key, part):
    counts = jax.random.randint(jax.random.fold_in(key, 21), (REQUESTS,), WINDOW // 2, WINDOW + 1)
    chosen = jax.random.randint(jax.random.fold_in(key, 22), (), 0, REQUESTS)
    return jnp.where(jnp.arange(REQUESTS) == chosen, WINDOW, counts).astype(jnp.int32)


def draw_cache_keys(key, part):
    source = jax.random.fold_in(key, 31)
    return jnp.clip(jax.random.normal(source, (REQUESTS, WINDOW, D), jnp.float32), -6.0, 6.0).astype(jnp.bfloat16)


def with_ends(values, own_key, least, high):
    spot = [jax.random.randint(jax.random.fold_in(own_key, axis), (), 0, length) for axis, length in enumerate(values.shape)]
    widest = values.shape.index(max(values.shape))
    next_to = spot[:widest] + [(spot[widest] + 1) % values.shape[widest]] + spot[widest + 1:]
    return values.at[tuple(spot)].set(least).at[tuple(next_to)].set(high)


def level_of(rng, dims, shards, smallest, high):
    gain, own = 1.0, jax.random.fold_in(rng, 6)
    for dim, parts in shards:
        steps = jnp.exp(jax.random.uniform(jax.random.fold_in(own, dim), (parts,), jnp.float32, smallest / len(shards), high / len(shards)))
        gain = gain * jnp.repeat(steps, dims[dim] // parts).reshape([-1 if axis == dim else 1 for axis in range(len(dims))])
    return gain


def gaussian(own_key, shape, scale, reach, shards=(), held_as=jnp.bfloat16):
    factor_of = level_of(own_key, shape, shards, -0.22, 0.18) if shards else 1.0
    values = jax.random.normal(own_key, shape, jnp.float32) * scale * factor_of
    return jnp.minimum(jnp.maximum(values, -reach), reach).astype(held_as)


def setup_inputs(seed: int = 0) -> dict:
    keys = jax.random.split(jax.random.key(seed), 15)
    tokens = gaussian(keys[0], (REQUESTS, SPAN, D), 1.0, 6.0, ((0, 4), (1, 2)))
    w_query = gaussian(keys[1], (D, D), D ** -0.5, 0.125, ((0, 8), (1, 4)))
    w_key = gaussian(keys[2], (D, D), D ** -0.5, 0.125, ((0, 8), (1, 4)))
    w_value = gaussian(keys[3], (D, D), D ** -0.5, 0.125, ((0, 8), (1, 4)))
    q_gain = jnp.clip(jnp.exp(math.log(4.0) - 1.3862944 * jax.random.uniform(keys[4], (D,), jnp.float32) ** level_of(keys[4], (D,), ((0, 4),), -0.2, 0.2)), 1.0, 4.0)
    k_gain = jnp.clip(jnp.exp(math.log(4.0) - 1.3862944 * jax.random.uniform(keys[5], (D,), jnp.float32) ** level_of(keys[5], (D,), ((0, 4),), -0.2, 0.2)), 1.0, 4.0)
    cache_keys = draw_cache_keys(jax.random.fold_in(keys[14], 71), 0)
    cache_values = gaussian(keys[7], (REQUESTS, WINDOW, D), 1.0, 6.0, ((0, 4), (1, 2), (2, 4)))
    sink_keys = gaussian(keys[8], (REQUESTS, SINKS, D), 4.0, 16.0, ((0, 4), (2, 4)))
    sink_values = gaussian(keys[9], (REQUESTS, SINKS, D), 1.0, 6.0, ((0, 4), (2, 4)))
    sink_pos = with_ends(jax.random.randint(keys[10], (REQUESTS, SINKS), 0, 2 * WINDOW), jax.random.fold_in(keys[10], 1), 0, (2 * WINDOW) - 1).astype(jnp.int32)
    cache_len = with_ends(jax.random.randint(keys[11], (REQUESTS,), 0, 8 * WINDOW + 1), jax.random.fold_in(keys[11], 1), 0, 8 * WINDOW).astype(jnp.int32)
    span_len = draw_span_len(jax.random.fold_in(keys[14], 71), 0)
    window_len = draw_window_len(jax.random.fold_in(keys[14], 71), 0)
    return dict(tokens=tokens, w_query=w_query, w_key=w_key, w_value=w_value, q_gain=q_gain, k_gain=k_gain, cache_keys=cache_keys, cache_values=cache_values, sink_keys=sink_keys, sink_values=sink_values, sink_pos=sink_pos, cache_len=cache_len, span_len=span_len, window_len=window_len)


rope_base = 500000.0
epsilon = 1e-06
lowest = -1e+30

def rotate_heads(vectors, positions):
    half_dim = vectors.shape[-1] // 2
    powers = jnp.arange(half_dim, dtype=jnp.float32) * (2.0 / vectors.shape[-1])
    inverse = rope_base ** (-powers)
    angles = positions.astype(jnp.float32)[:, None] * inverse[None, :]
    cosine = jnp.cos(angles)[:, None, :]
    sine_part = jnp.sin(angles)[:, None, :]
    leading = vectors[..., :half_dim]
    trailing = vectors[..., half_dim:]
    return jnp.concatenate([leading * cosine - trailing * sine_part, trailing * cosine + leading * sine_part], axis=-1)

def normalize_rotate(projected, squares, feature_gain, positions, model_width, head_size):
    factor = lax.rsqrt(squares / model_width + epsilon)
    normed = projected * factor[:, None] * feature_gain[None, :]
    shaped = normed.reshape(projected.shape[0], projected.shape[1] // head_size, head_size)
    return rotate_heads(shaped, positions).reshape(projected.shape).astype(jnp.bfloat16)

def reference(tokens, w_query, w_key, w_value, q_gain, k_gain, cache_keys, cache_values, sink_keys, sink_values, sink_pos, cache_len, span_len, window_len):
    token_rows = tokens.reshape(REQUESTS * SPAN, D)
    q_raw = jnp.dot(token_rows, w_query, preferred_element_type=jnp.float32)
    k_raw = jnp.dot(token_rows, w_key, preferred_element_type=jnp.float32)
    v_new = jnp.dot(token_rows, w_value, preferred_element_type=jnp.float32).astype(jnp.bfloat16)
    offsets = jnp.arange(SPAN, dtype=jnp.int32)
    positions = (cache_len[:, None] + offsets[None, :]).reshape(-1).astype(jnp.int32)
    q_rot = normalize_rotate(q_raw, lax.optimization_barrier(jnp.sum(q_raw * q_raw, axis=1)), q_gain, positions, D, HEAD_DIM).reshape(REQUESTS, SPAN, D)
    k_rot = normalize_rotate(k_raw, lax.optimization_barrier(jnp.sum(k_raw * k_raw, axis=1)), k_gain, positions, D, HEAD_DIM).reshape(REQUESTS, SPAN, D)
    v_new = v_new.reshape(REQUESTS, SPAN, D)
    slot_index = jnp.arange(WINDOW, dtype=jnp.int32)
    scaling = HEAD_DIM ** (-0.5)

    def one_request(operands):
        query, key_new, value_new, cache_k, cache_v, sink_k, sink_v, sink_at, length_now, live_count, window_now = operands
        query_pos = length_now + offsets
        slot_pos = length_now - 1 - jnp.mod(length_now - 1 - slot_index, WINDOW)
        edge_pos = query_pos - window_now
        sink_mask = sink_at[None, :] <= edge_pos[:, None]
        slot_mask = (slot_pos[None, :] >= 0) & (slot_pos[None, :] > edge_pos[:, None])
        span_mask = offsets[None, :] <= offsets[:, None]
        allowed = jnp.concatenate([sink_mask, slot_mask, span_mask], axis=1)
        all_keys = jnp.concatenate([sink_k, cache_k, key_new], axis=0).reshape(-1, HEADS, HEAD_DIM)
        all_values = jnp.concatenate([sink_v, cache_v, value_new], axis=0).reshape(-1, HEADS, HEAD_DIM)
        query_heads = query.reshape(SPAN, HEADS, HEAD_DIM)

        def one_head(head_index):
            query_head = query_heads[:, head_index]
            key_head = all_keys[:, head_index]
            value_head = all_values[:, head_index]
            scores = jnp.dot(query_head, key_head.T, preferred_element_type=jnp.float32) * scaling
            highest = lax.optimization_barrier(jnp.max(jnp.where(allowed, scores, lowest), axis=1))
            weights = jnp.where(allowed, jnp.exp(scores - highest[:, None]), 0.0)
            totals = lax.optimization_barrier(jnp.sum(weights, axis=1))
            summed = jnp.dot(weights.astype(jnp.bfloat16), value_head, preferred_element_type=jnp.float32)
            return summed / totals[:, None]
        heads_out = lax.map(one_head, jnp.arange(HEADS, dtype=jnp.int32))
        live_rows = offsets < live_count
        result = jnp.where(live_rows[:, None, None], jnp.transpose(heads_out, (1, 0, 2)), 0.0)
        return result.reshape(SPAN, D).astype(jnp.bfloat16)
    return lax.map(one_request, (q_rot, k_rot, v_new, cache_keys, cache_values, sink_keys, sink_values, sink_pos, cache_len, span_len, window_len))
```

```python
import functools

import jax
import jax.numpy as jnp
from jax import lax
from jax.experimental import pallas as pl
from jax.experimental.pallas import tpu as pltpu
from jax.sharding import PartitionSpec as P

D = 2048
HEAD_DIM = 128
WINDOW = 4096
SINKS = 4


rope_base = 500000.0
epsilon = 1e-06
lowest = -1e30


def rotate_heads(vectors, positions):
    half_dim = vectors.shape[-1] // 2
    powers = jnp.arange(half_dim, dtype=jnp.float32) * (2.0 / vectors.shape[-1])
    inverse = rope_base ** (-powers)
    angles = positions.astype(jnp.float32)[:, None] * inverse[None, :]
    cosine = jnp.cos(angles)[:, None, :]
    sine_part = jnp.sin(angles)[:, None, :]
    leading = vectors[..., :half_dim]
    trailing = vectors[..., half_dim:]
    return jnp.concatenate(
        [leading * cosine - trailing * sine_part, trailing * cosine + leading * sine_part], axis=-1
    )


def normalize_rotate(projected, squares, feature_gain, positions, model_width, head_size):
    factor = lax.rsqrt(squares / model_width + epsilon)
    normed = projected * factor[:, None] * feature_gain[None, :]
    shaped = normed.reshape(projected.shape[0], projected.shape[1] // head_size, head_size)
    return rotate_heads(shaped, positions).reshape(projected.shape).astype(jnp.bfloat16)


def attention_kernel(
    len_ref, win_ref, seq_ref, q_ref, ck_ref, cv_ref, nk_ref, nv_ref, o_ref, m_ref, l_ref, *, scaling
):
    r = pl.program_id(0)
    length_now = len_ref[r]
    window_now = win_ref[r]
    seq_index = seq_ref[0]
    queries = q_ref[0]
    rows, slots, span_local = queries.shape[0], ck_ref.shape[1], nk_ref.shape[1]
    dims = (((1,), (1,)), ((), ()))
    cache_scores = (
        lax.dot_general(queries, ck_ref[0], dims, preferred_element_type=jnp.float32) * scaling
    )
    span_scores = (
        lax.dot_general(queries, nk_ref[0], dims, preferred_element_type=jnp.float32) * scaling
    )
    row_c = lax.broadcasted_iota(jnp.int32, (rows, slots), 0)
    slot = lax.broadcasted_iota(jnp.int32, (rows, slots), 1) + seq_index * slots
    edge = length_now + row_c - window_now
    slot_pos = length_now - 1 - ((length_now - 1 - slot) & (WINDOW - 1))
    cache_ok = (slot_pos >= 0) & (slot_pos > edge)
    row_s = lax.broadcasted_iota(jnp.int32, (rows, span_local), 0)
    key_s = lax.broadcasted_iota(jnp.int32, (rows, span_local), 1) + seq_index * span_local
    span_ok = key_s <= row_s
    highest = jnp.maximum(
        jnp.max(jnp.where(cache_ok, cache_scores, lowest), axis=1, keepdims=True),
        jnp.max(jnp.where(span_ok, span_scores, lowest), axis=1, keepdims=True),
    )
    cache_w = jnp.where(cache_ok, jnp.exp(cache_scores - highest), 0.0)
    span_w = jnp.where(span_ok, jnp.exp(span_scores - highest), 0.0)
    totals = jnp.sum(cache_w, axis=1, keepdims=True) + jnp.sum(span_w, axis=1, keepdims=True)
    summed = jnp.dot(
        cache_w.astype(jnp.bfloat16), cv_ref[0], preferred_element_type=jnp.float32
    ) + jnp.dot(span_w.astype(jnp.bfloat16), nv_ref[0], preferred_element_type=jnp.float32)
    o_ref[0, 0] = summed
    m_ref[0, 0] = highest
    l_ref[0, 0] = totals


def local_attention(q_whole, cache_keys, cache_values, k_rot, v_new, cache_len, window_len, seq_index):
    req_local, span_total, local_cols = q_whole.shape
    heads_local = local_cols // HEAD_DIM
    slot_local = cache_keys.shape[1]
    span_local = k_rot.shape[1]
    kernel = functools.partial(attention_kernel, scaling=HEAD_DIM ** (-0.5))
    grid_spec = pltpu.PrefetchScalarGridSpec(
        num_scalar_prefetch=3,
        grid=(req_local, heads_local),
        in_specs=[
            pl.BlockSpec((1, span_total, HEAD_DIM), lambda r, h, *_: (r, 0, h)),
            pl.BlockSpec((1, slot_local, HEAD_DIM), lambda r, h, *_: (r, 0, h)),
            pl.BlockSpec((1, slot_local, HEAD_DIM), lambda r, h, *_: (r, 0, h)),
            pl.BlockSpec((1, span_local, HEAD_DIM), lambda r, h, *_: (r, 0, h)),
            pl.BlockSpec((1, span_local, HEAD_DIM), lambda r, h, *_: (r, 0, h)),
        ],
        out_specs=[
            pl.BlockSpec((1, 1, span_total, HEAD_DIM), lambda r, h, *_: (r, h, 0, 0)),
            pl.BlockSpec((1, 1, span_total, 1), lambda r, h, *_: (r, h, 0, 0)),
            pl.BlockSpec((1, 1, span_total, 1), lambda r, h, *_: (r, h, 0, 0)),
        ],
    )
    return pl.pallas_call(
        kernel,
        grid_spec=grid_spec,
        out_shape=[
            jax.ShapeDtypeStruct((req_local, heads_local, span_total, HEAD_DIM), jnp.float32),
            jax.ShapeDtypeStruct((req_local, heads_local, span_total, 1), jnp.float32),
            jax.ShapeDtypeStruct((req_local, heads_local, span_total, 1), jnp.float32),
        ],
    )(
        cache_len,
        window_len,
        jnp.reshape(seq_index, (1,)).astype(jnp.int32),
        q_whole,
        cache_keys,
        cache_values,
        k_rot,
        v_new,
    )


def on_device(
    tokens,
    w_query,
    w_key,
    w_value,
    q_gain,
    k_gain,
    cache_keys,
    cache_values,
    sink_keys,
    sink_values,
    sink_pos,
    cache_len,
    span_len,
    window_len,
):
    req_local, span_local, model_width = tokens.shape
    local_cols = w_query.shape[1]
    heads_local = local_cols // HEAD_DIM
    seq_count = lax.axis_size("seq")
    seq_index = lax.axis_index("seq")
    span_total = span_local * seq_count
    scaling = HEAD_DIM ** (-0.5)
    token_rows = tokens.reshape(req_local * span_local, model_width)
    w_all = lax.all_gather(
        jnp.concatenate([w_query, w_key, w_value], axis=1), ("req", "seq"), axis=0, tiled=True
    )
    proj = jnp.dot(token_rows, w_all, preferred_element_type=jnp.float32)
    q_proj = proj[:, :local_cols]
    k_proj = proj[:, local_cols : 2 * local_cols]
    v_proj = proj[:, 2 * local_cols :]
    q_squares, k_squares = lax.psum(
        (jnp.sum(q_proj * q_proj, axis=1), jnp.sum(k_proj * k_proj, axis=1)), "tp"
    )
    offsets = seq_index * span_local + jnp.arange(span_local, dtype=jnp.int32)
    positions = (cache_len[:, None] + offsets[None, :]).reshape(-1)
    q_local = normalize_rotate(q_proj, q_squares, q_gain, positions, D, HEAD_DIM).reshape(
        req_local, span_local, local_cols
    )
    k_rot = normalize_rotate(k_proj, k_squares, k_gain, positions, D, HEAD_DIM).reshape(
        req_local, span_local, local_cols
    )
    v_new = v_proj.astype(jnp.bfloat16).reshape(req_local, span_local, local_cols)
    q_whole = lax.all_gather(q_local, "seq", axis=1, tiled=True)
    part_sum, part_high, part_total = local_attention(
        q_whole, cache_keys, cache_values, k_rot, v_new, cache_len, window_len, seq_index
    )
    stats = jnp.concatenate([part_high, part_total], axis=3)
    got_sum = lax.all_to_all(
        part_sum.reshape(req_local, heads_local, seq_count, span_local, HEAD_DIM),
        "seq",
        split_axis=2,
        concat_axis=2,
        tiled=True,
    )
    got_stats = lax.all_to_all(
        stats.reshape(req_local, heads_local, seq_count, span_local, 2),
        "seq",
        split_axis=2,
        concat_axis=2,
        tiled=True,
    )
    got_high = got_stats[..., 0]
    got_total = got_stats[..., 1]
    own_heads = q_local.reshape(req_local, span_local, heads_local, HEAD_DIM)
    sink_heads = sink_keys.reshape(req_local, SINKS, heads_local, HEAD_DIM)
    sink_vheads = sink_values.reshape(req_local, SINKS, heads_local, HEAD_DIM)
    sink_scores = (
        jnp.einsum("rqhd,rshd->rhqs", own_heads, sink_heads, preferred_element_type=jnp.float32)
        * scaling
    )
    sink_edge = cache_len[:, None] + offsets[None, :] - window_len[:, None]
    sink_allowed = sink_pos[:, None, None, :] <= sink_edge[:, None, :, None]
    sink_high = jnp.max(jnp.where(sink_allowed, sink_scores, lowest), axis=3)
    sink_weights = jnp.where(sink_allowed, jnp.exp(sink_scores - sink_high[..., None]), 0.0)
    sink_total = jnp.sum(sink_weights, axis=3)
    sink_sum = jnp.einsum(
        "rhqs,rshd->rhqd",
        sink_weights.astype(jnp.bfloat16),
        sink_vheads,
        preferred_element_type=jnp.float32,
    )
    all_high = jnp.concatenate([got_high, sink_high[:, :, None]], axis=2)
    all_total = jnp.concatenate([got_total, sink_total[:, :, None]], axis=2)
    all_parts = jnp.concatenate([got_sum, sink_sum[:, :, None]], axis=2)
    peak_value = jnp.max(all_high, axis=2, keepdims=True)
    factor = jnp.exp(all_high - peak_value)
    denominator = jnp.sum(all_total * factor, axis=2)
    numerator = jnp.sum(all_parts * factor[..., None], axis=2)
    live_rows = (offsets[None, :] < span_len[:, None])[:, None, :]
    safe_total = jnp.where(live_rows, denominator, 1.0)
    mixed = jnp.where(live_rows[..., None], numerator / safe_total[..., None], 0.0)
    return (
        mixed.transpose(0, 2, 1, 3).reshape(req_local, span_local, local_cols).astype(jnp.bfloat16)
    )


def solution(mesh):
    placed = (
        P("req", "seq", None),
        P(("req", "seq"), "tp"),
        P(("req", "seq"), "tp"),
        P(("req", "seq"), "tp"),
        P("tp"),
        P("tp"),
        P("req", "seq", "tp"),
        P("req", "seq", "tp"),
        P("req", None, "tp"),
        P("req", None, "tp"),
        P("req", None),
        P("req"),
        P("req"),
        P("req"),
    )
    return jax.shard_map(
        on_device, mesh=mesh, in_specs=placed, out_specs=P("req", "seq", "tp"), check_vma=False
    )
```

```python
import functools

import jax
import jax.numpy as jnp
from jax import lax
from jax.experimental import pallas as pl
from jax.experimental.pallas import tpu as pltpu
from jax.sharding import PartitionSpec as P

D = 2048
HEAD_DIM = 128
WINDOW = 4096
SINKS = 4


rope_base = 500000.0
epsilon = 1e-06
lowest = -1e30


def rotate_heads(vectors, positions):
    half_dim = vectors.shape[-1] // 2
    powers = jnp.arange(half_dim, dtype=jnp.float32) * (2.0 / vectors.shape[-1])
    inverse = rope_base ** (-powers)
    angles = positions.astype(jnp.float32)[:, None] * inverse[None, :]
    cosine = jnp.cos(angles)[:, None, :]
    sine_part = jnp.sin(angles)[:, None, :]
    leading = vectors[..., :half_dim]
    trailing = vectors[..., half_dim:]
    return jnp.concatenate(
        [leading * cosine - trailing * sine_part, trailing * cosine + leading * sine_part], axis=-1
    )


def normalize_rotate(projected, squares, feature_gain, positions, model_width, head_size):
    factor = lax.rsqrt(squares / model_width + epsilon)
    normed = projected * factor[:, None] * feature_gain[None, :]
    shaped = normed.reshape(projected.shape[0], projected.shape[1] // head_size, head_size)
    return rotate_heads(shaped, positions).reshape(projected.shape).astype(jnp.bfloat16)


def cache_kernel(len_ref, win_ref, seq_ref, q_ref, ck_ref, cv_ref, o_ref, m_ref, l_ref, *, scaling):
    r = pl.program_id(0)
    length_now = len_ref[r]
    window_now = win_ref[r]
    seq_index = seq_ref[0]
    seq_count, _, span_local, _ = q_ref.shape
    slots = ck_ref.shape[1]
    keys = ck_ref[0]
    values = cv_ref[0]
    dims = (((1,), (1,)), ((), ()))
    row = lax.broadcasted_iota(jnp.int32, (span_local, slots), 0)
    slot = lax.broadcasted_iota(jnp.int32, (span_local, slots), 1) + seq_index * slots
    slot_pos = length_now - 1 - ((length_now - 1 - slot) & (WINDOW - 1))
    for shift in range(seq_count):
        owner = (seq_index - shift + seq_count) % seq_count
        scores = (
            lax.dot_general(q_ref[shift, 0], keys, dims, preferred_element_type=jnp.float32)
            * scaling
        )
        edge = length_now + owner * span_local + row - window_now
        allowed = (slot_pos >= 0) & (slot_pos > edge)
        highest = jnp.max(jnp.where(allowed, scores, lowest), axis=1, keepdims=True)
        weights = jnp.where(allowed, jnp.exp(scores - highest), 0.0)
        o_ref[shift, 0, 0] = jnp.dot(
            weights.astype(jnp.bfloat16), values, preferred_element_type=jnp.float32
        )
        m_ref[shift, 0, 0] = highest
        l_ref[shift, 0, 0] = jnp.sum(weights, axis=1, keepdims=True)


def cache_attention(q_parts, cache_keys, cache_values, cache_len, window_len, seq_index):
    seq_count, req_local, span_local, local_cols = q_parts.shape
    heads_local = local_cols // HEAD_DIM
    slot_local = cache_keys.shape[1]
    kernel = functools.partial(cache_kernel, scaling=HEAD_DIM ** (-0.5))
    part = (seq_count, 1, 1, span_local)
    grid_spec = pltpu.PrefetchScalarGridSpec(
        num_scalar_prefetch=3,
        grid=(req_local, heads_local),
        in_specs=[
            pl.BlockSpec((seq_count, 1, span_local, HEAD_DIM), lambda r, h, *_: (0, r, 0, h)),
            pl.BlockSpec((1, slot_local, HEAD_DIM), lambda r, h, *_: (r, 0, h)),
            pl.BlockSpec((1, slot_local, HEAD_DIM), lambda r, h, *_: (r, 0, h)),
        ],
        out_specs=[
            pl.BlockSpec(part + (HEAD_DIM,), lambda r, h, *_: (0, r, h, 0, 0)),
            pl.BlockSpec(part + (1,), lambda r, h, *_: (0, r, h, 0, 0)),
            pl.BlockSpec(part + (1,), lambda r, h, *_: (0, r, h, 0, 0)),
        ],
    )
    shape = (seq_count, req_local, heads_local, span_local)
    return pl.pallas_call(
        kernel,
        grid_spec=grid_spec,
        out_shape=[
            jax.ShapeDtypeStruct(shape + (HEAD_DIM,), jnp.float32),
            jax.ShapeDtypeStruct(shape + (1,), jnp.float32),
            jax.ShapeDtypeStruct(shape + (1,), jnp.float32),
        ],
    )(
        cache_len,
        window_len,
        jnp.reshape(seq_index, (1,)).astype(jnp.int32),
        q_parts,
        cache_keys,
        cache_values,
    )


def span_kernel(
    len_ref,
    win_ref,
    seq_ref,
    live_ref,
    sink_pos_ref,
    q_ref,
    nk_ref,
    nv_ref,
    sk_ref,
    sv_ref,
    ps_ref,
    pst_ref,
    out_ref,
    *,
    scaling,
):
    r = pl.program_id(0)
    length_now = len_ref[r]
    window_now = win_ref[r]
    seq_index = seq_ref[0]
    live_count = live_ref[r]
    seq_count, _, span_local, _ = nk_ref.shape
    queries = q_ref[0]
    dims = (((1,), (1,)), ((), ()))
    row = lax.broadcasted_iota(jnp.int32, (span_local, span_local), 0) + seq_index * span_local
    col = lax.broadcasted_iota(jnp.int32, (span_local, span_local), 1)
    span_scores, span_ok = [], []
    for shift in range(seq_count):
        owner = (seq_index - shift + seq_count) % seq_count
        span_scores.append(
            lax.dot_general(queries, nk_ref[shift, 0], dims, preferred_element_type=jnp.float32)
            * scaling
        )
        span_ok.append(owner * span_local + col <= row)
    query_f = queries.astype(jnp.float32)
    row_1 = lax.broadcasted_iota(jnp.int32, (span_local, 1), 0) + seq_index * span_local
    edge = length_now + row_1 - window_now
    sink_scores, sink_ok = [], []
    for sink in range(SINKS):
        key_f = sk_ref[0, sink : sink + 1, :].astype(jnp.float32)
        sink_scores.append(jnp.sum(query_f * key_f, axis=1, keepdims=True) * scaling)
        sink_ok.append(sink_pos_ref[r * SINKS + sink] <= edge)
    part_high = pst_ref[:, 0, 0, :, 0:1]
    part_total = pst_ref[:, 0, 0, :, 1:2]
    peak = jnp.max(part_high, axis=0)
    for scores, ok in zip(span_scores + sink_scores, span_ok + sink_ok):
        peak = jnp.maximum(peak, jnp.max(jnp.where(ok, scores, lowest), axis=1, keepdims=True))
    factor = jnp.exp(part_high - peak[None])
    denominator = jnp.sum(part_total * factor, axis=0)
    numerator = jnp.sum(ps_ref[:, 0, 0] * factor, axis=0)
    for shift in range(seq_count):
        weights = jnp.where(span_ok[shift], jnp.exp(span_scores[shift] - peak), 0.0)
        denominator = denominator + jnp.sum(weights, axis=1, keepdims=True)
        numerator = numerator + jnp.dot(
            weights.astype(jnp.bfloat16), nv_ref[shift, 0], preferred_element_type=jnp.float32
        )
    for sink in range(SINKS):
        weights = jnp.where(sink_ok[sink], jnp.exp(sink_scores[sink] - peak), 0.0)
        denominator = denominator + weights
        value_f = sv_ref[0, sink : sink + 1, :].astype(jnp.float32)
        numerator = numerator + weights.astype(jnp.bfloat16).astype(jnp.float32) * value_f
    live = row_1 < live_count
    safe = jnp.where(live, denominator, 1.0)
    out_ref[0] = jnp.where(live, numerator / safe, 0.0).astype(out_ref.dtype)


def span_attention(
    q_local, kv_parts, sink_keys, sink_values, parts_sum, parts_stats, scalars
):
    req_local, span_local, local_cols = q_local.shape
    seq_count = kv_parts.shape[0]
    heads_local = local_cols // HEAD_DIM
    kernel = functools.partial(span_kernel, scaling=HEAD_DIM ** (-0.5))
    part = (seq_count, 1, 1, span_local)
    grid_spec = pltpu.PrefetchScalarGridSpec(
        num_scalar_prefetch=5,
        grid=(req_local, heads_local),
        in_specs=[
            pl.BlockSpec((1, span_local, HEAD_DIM), lambda r, h, *_: (r, 0, h)),
            pl.BlockSpec((seq_count, 1, span_local, HEAD_DIM), lambda r, h, *_: (0, r, 0, h)),
            pl.BlockSpec(
                (seq_count, 1, span_local, HEAD_DIM),
                lambda r, h, *_: (0, r, 0, h + heads_local),
            ),
            pl.BlockSpec((1, SINKS, HEAD_DIM), lambda r, h, *_: (r, 0, h)),
            pl.BlockSpec((1, SINKS, HEAD_DIM), lambda r, h, *_: (r, 0, h)),
            pl.BlockSpec(part + (HEAD_DIM,), lambda r, h, *_: (0, r, h, 0, 0)),
            pl.BlockSpec(part + (2,), lambda r, h, *_: (0, r, h, 0, 0)),
        ],
        out_specs=pl.BlockSpec((1, span_local, HEAD_DIM), lambda r, h, *_: (r, 0, h)),
    )
    return pl.pallas_call(
        kernel,
        grid_spec=grid_spec,
        out_shape=jax.ShapeDtypeStruct((req_local, span_local, local_cols), jnp.bfloat16),
    )(*scalars, q_local, kv_parts, kv_parts, sink_keys, sink_values, parts_sum, parts_stats)


def shifted(x, axis_name, shift):
    count = lax.axis_size(axis_name)
    if shift % count == 0:
        return x
    return lax.ppermute(x, axis_name, [(a, (a + shift) % count) for a in range(count)])


def tp_sum(x):
    count = lax.axis_size("tp")
    assert count & (count - 1) == 0
    bit = 1
    while bit < count:
        x = x + lax.ppermute(x, "tp", [(a, a ^ bit) for a in range(count)])
        bit *= 2
    return x


def on_device(
    tokens,
    w_query,
    w_key,
    w_value,
    q_gain,
    k_gain,
    cache_keys,
    cache_values,
    sink_keys,
    sink_values,
    sink_pos,
    cache_len,
    span_len,
    window_len,
):
    req_local, span_local, model_width = tokens.shape
    local_cols = w_query.shape[1]
    seq_count = lax.axis_size("seq")
    seq_index = lax.axis_index("seq")
    token_rows = tokens.reshape(req_local * span_local, model_width)
    offsets = seq_index * span_local + jnp.arange(span_local, dtype=jnp.int32)
    positions = (cache_len[:, None] + offsets[None, :]).reshape(-1)
    wq_all = lax.all_gather(w_query, ("req", "seq"), axis=0, tiled=True)
    wkv_all = lax.all_gather(
        jnp.concatenate([w_key, w_value], axis=1), ("req", "seq"), axis=0, tiled=True
    )
    q_proj = jnp.dot(token_rows, wq_all, preferred_element_type=jnp.float32)
    q_squares = tp_sum(jnp.sum(q_proj * q_proj, axis=1))
    q_local = normalize_rotate(q_proj, q_squares, q_gain, positions, D, HEAD_DIM).reshape(
        req_local, span_local, local_cols
    )
    q_parts = jnp.stack([shifted(q_local, "seq", shift) for shift in range(seq_count)])
    c_sum, c_high, c_total = cache_attention(
        q_parts, cache_keys, cache_values, cache_len, window_len, seq_index
    )
    wkv_all, c_sum, c_high, c_total = lax.optimization_barrier((wkv_all, c_sum, c_high, c_total))
    c_stats = jnp.concatenate([c_high, c_total], axis=-1)
    parts_sum = jnp.stack([shifted(c_sum[s], "seq", -s) for s in range(seq_count)])
    parts_stats = jnp.stack([shifted(c_stats[s], "seq", -s) for s in range(seq_count)])
    kv_proj = jnp.dot(token_rows, wkv_all, preferred_element_type=jnp.float32)
    k_proj = kv_proj[:, :local_cols]
    k_squares = tp_sum(jnp.sum(k_proj * k_proj, axis=1))
    k_rot = normalize_rotate(k_proj, k_squares, k_gain, positions, D, HEAD_DIM)
    v_new = kv_proj[:, local_cols:].astype(jnp.bfloat16)
    kv_new = jnp.concatenate([k_rot, v_new], axis=1).reshape(req_local, span_local, 2 * local_cols)
    kv_parts = jnp.stack([shifted(kv_new, "seq", shift) for shift in range(seq_count)])
    scalars = (
        cache_len,
        window_len,
        jnp.reshape(seq_index, (1,)).astype(jnp.int32),
        span_len,
        sink_pos.reshape(-1),
    )
    return span_attention(
        q_local, kv_parts, sink_keys, sink_values, parts_sum, parts_stats, scalars
    )


def solution(mesh):
    placed = (
        P("req", "seq", None),
        P(("req", "seq"), "tp"),
        P(("req", "seq"), "tp"),
        P(("req", "seq"), "tp"),
        P("tp"),
        P("tp"),
        P("req", "seq", "tp"),
        P("req", "seq", "tp"),
        P("req", None, "tp"),
        P("req", None, "tp"),
        P("req", None),
        P("req"),
        P("req"),
        P("req"),
    )
    return jax.shard_map(
        on_device, mesh=mesh, in_specs=placed, out_specs=P("req", "seq", "tp"), check_vma=False
    )
```

```python
import functools

import jax
import jax.numpy as jnp
from jax import lax
from jax.experimental import pallas as pl
from jax.experimental.pallas import tpu as pltpu
from jax.sharding import PartitionSpec as P

D = 2048
HEAD_DIM = 128
WINDOW = 4096
SINKS = 4


rope_base = 500000.0
epsilon = 1e-06
lowest = -1e30


def rotate_heads(vectors, positions):
    half_dim = vectors.shape[-1] // 2
    powers = jnp.arange(half_dim, dtype=jnp.float32) * (2.0 / vectors.shape[-1])
    inverse = rope_base ** (-powers)
    angles = positions.astype(jnp.float32)[:, None] * inverse[None, :]
    cosine = jnp.cos(angles)[:, None, :]
    sine_part = jnp.sin(angles)[:, None, :]
    leading = vectors[..., :half_dim]
    trailing = vectors[..., half_dim:]
    return jnp.concatenate(
        [leading * cosine - trailing * sine_part, trailing * cosine + leading * sine_part], axis=-1
    )


def normalize_rotate(projected, squares, feature_gain, positions, model_width, head_size):
    factor = lax.rsqrt(squares / model_width + epsilon)
    normed = projected * factor[:, None] * feature_gain[None, :]
    shaped = normed.reshape(projected.shape[0], projected.shape[1] // head_size, head_size)
    return rotate_heads(shaped, positions).reshape(projected.shape).astype(jnp.bfloat16)


def cache_kernel(len_ref, win_ref, seq_ref, q_ref, ck_ref, cv_ref, o_ref, m_ref, l_ref, *, scaling):
    r = pl.program_id(0)
    length_now = len_ref[r]
    window_now = win_ref[r]
    seq_index = seq_ref[0]
    seq_count, _, span_local, _ = q_ref.shape
    slots = ck_ref.shape[1]
    keys = ck_ref[0]
    values = cv_ref[0]
    dims = (((1,), (1,)), ((), ()))
    row = lax.broadcasted_iota(jnp.int32, (span_local, slots), 0)
    slot = lax.broadcasted_iota(jnp.int32, (span_local, slots), 1) + seq_index * slots
    slot_pos = length_now - 1 - ((length_now - 1 - slot) & (WINDOW - 1))
    for shift in range(seq_count):
        owner = (seq_index - shift + seq_count) % seq_count
        scores = (
            lax.dot_general(q_ref[shift, 0], keys, dims, preferred_element_type=jnp.float32)
            * scaling
        )
        edge = length_now + owner * span_local + row - window_now
        allowed = (slot_pos >= 0) & (slot_pos > edge)
        highest = jnp.max(jnp.where(allowed, scores, lowest), axis=1, keepdims=True)
        weights = jnp.where(allowed, jnp.exp(scores - highest), 0.0)
        o_ref[shift, 0, 0] = jnp.dot(
            weights.astype(jnp.bfloat16), values, preferred_element_type=jnp.float32
        )
        m_ref[shift, 0, 0] = highest
        l_ref[shift, 0, 0] = jnp.sum(weights, axis=1, keepdims=True)


def cache_attention(q_parts, cache_keys, cache_values, cache_len, window_len, seq_index):
    seq_count, req_local, span_local, local_cols = q_parts.shape
    heads_local = local_cols // HEAD_DIM
    slot_local = cache_keys.shape[1]
    kernel = functools.partial(cache_kernel, scaling=HEAD_DIM ** (-0.5))
    part = (seq_count, 1, 1, span_local)
    grid_spec = pltpu.PrefetchScalarGridSpec(
        num_scalar_prefetch=3,
        grid=(req_local, heads_local),
        in_specs=[
            pl.BlockSpec((seq_count, 1, span_local, HEAD_DIM), lambda r, h, *_: (0, r, 0, h)),
            pl.BlockSpec((1, slot_local, HEAD_DIM), lambda r, h, *_: (r, 0, h)),
            pl.BlockSpec((1, slot_local, HEAD_DIM), lambda r, h, *_: (r, 0, h)),
        ],
        out_specs=[
            pl.BlockSpec(part + (HEAD_DIM,), lambda r, h, *_: (0, r, h, 0, 0)),
            pl.BlockSpec(part + (1,), lambda r, h, *_: (0, r, h, 0, 0)),
            pl.BlockSpec(part + (1,), lambda r, h, *_: (0, r, h, 0, 0)),
        ],
    )
    shape = (seq_count, req_local, heads_local, span_local)
    return pl.pallas_call(
        kernel,
        grid_spec=grid_spec,
        out_shape=[
            jax.ShapeDtypeStruct(shape + (HEAD_DIM,), jnp.float32),
            jax.ShapeDtypeStruct(shape + (1,), jnp.float32),
            jax.ShapeDtypeStruct(shape + (1,), jnp.float32),
        ],
    )(
        cache_len,
        window_len,
        jnp.reshape(seq_index, (1,)).astype(jnp.int32),
        q_parts,
        cache_keys,
        cache_values,
    )


def span_kernel(
    len_ref,
    win_ref,
    seq_ref,
    live_ref,
    sink_pos_ref,
    q_ref,
    nk_ref,
    nv_ref,
    sk_ref,
    sv_ref,
    ps_ref,
    pst_ref,
    out_ref,
    *,
    scaling,
):
    r = pl.program_id(0)
    length_now = len_ref[r]
    window_now = win_ref[r]
    seq_index = seq_ref[0]
    live_count = live_ref[r]
    seq_count, _, span_local, _ = nk_ref.shape
    queries = q_ref[0]
    dims = (((1,), (1,)), ((), ()))
    row = lax.broadcasted_iota(jnp.int32, (span_local, span_local), 0) + seq_index * span_local
    col = lax.broadcasted_iota(jnp.int32, (span_local, span_local), 1)
    span_scores, span_ok = [], []
    for shift in range(seq_count):
        owner = (seq_index - shift + seq_count) % seq_count
        span_scores.append(
            lax.dot_general(queries, nk_ref[shift, 0], dims, preferred_element_type=jnp.float32)
            * scaling
        )
        span_ok.append(owner * span_local + col <= row)
    query_f = queries.astype(jnp.float32)
    row_1 = lax.broadcasted_iota(jnp.int32, (span_local, 1), 0) + seq_index * span_local
    edge = length_now + row_1 - window_now
    sink_scores, sink_ok = [], []
    for sink in range(SINKS):
        key_f = sk_ref[0, sink : sink + 1, :].astype(jnp.float32)
        sink_scores.append(jnp.sum(query_f * key_f, axis=1, keepdims=True) * scaling)
        sink_ok.append(sink_pos_ref[r * SINKS + sink] <= edge)
    part_high = pst_ref[:, 0, 0, :, 0:1]
    part_total = pst_ref[:, 0, 0, :, 1:2]
    peak = jnp.max(part_high, axis=0)
    for scores, ok in zip(span_scores + sink_scores, span_ok + sink_ok):
        peak = jnp.maximum(peak, jnp.max(jnp.where(ok, scores, lowest), axis=1, keepdims=True))
    factor = jnp.exp(part_high - peak[None])
    denominator = jnp.sum(part_total * factor, axis=0)
    numerator = jnp.sum(ps_ref[:, 0, 0] * factor, axis=0)
    for shift in range(seq_count):
        weights = jnp.where(span_ok[shift], jnp.exp(span_scores[shift] - peak), 0.0)
        denominator = denominator + jnp.sum(weights, axis=1, keepdims=True)
        numerator = numerator + jnp.dot(
            weights.astype(jnp.bfloat16), nv_ref[shift, 0], preferred_element_type=jnp.float32
        )
    for sink in range(SINKS):
        weights = jnp.where(sink_ok[sink], jnp.exp(sink_scores[sink] - peak), 0.0)
        denominator = denominator + weights
        value_f = sv_ref[0, sink : sink + 1, :].astype(jnp.float32)
        numerator = numerator + weights.astype(jnp.bfloat16).astype(jnp.float32) * value_f
    live = row_1 < live_count
    safe = jnp.where(live, denominator, 1.0)
    out_ref[0] = jnp.where(live, numerator / safe, 0.0).astype(out_ref.dtype)


def span_attention(
    q_local, kv_parts, sink_keys, sink_values, parts_sum, parts_stats, scalars
):
    req_local, span_local, local_cols = q_local.shape
    seq_count = kv_parts.shape[0]
    heads_local = local_cols // HEAD_DIM
    kernel = functools.partial(span_kernel, scaling=HEAD_DIM ** (-0.5))
    part = (seq_count, 1, 1, span_local)
    grid_spec = pltpu.PrefetchScalarGridSpec(
        num_scalar_prefetch=5,
        grid=(req_local, heads_local),
        in_specs=[
            pl.BlockSpec((1, span_local, HEAD_DIM), lambda r, h, *_: (r, 0, h)),
            pl.BlockSpec((seq_count, 1, span_local, HEAD_DIM), lambda r, h, *_: (0, r, 0, h)),
            pl.BlockSpec(
                (seq_count, 1, span_local, HEAD_DIM),
                lambda r, h, *_: (0, r, 0, h + heads_local),
            ),
            pl.BlockSpec((1, SINKS, HEAD_DIM), lambda r, h, *_: (r, 0, h)),
            pl.BlockSpec((1, SINKS, HEAD_DIM), lambda r, h, *_: (r, 0, h)),
            pl.BlockSpec(part + (HEAD_DIM,), lambda r, h, *_: (0, r, h, 0, 0)),
            pl.BlockSpec(part + (2,), lambda r, h, *_: (0, r, h, 0, 0)),
        ],
        out_specs=pl.BlockSpec((1, span_local, HEAD_DIM), lambda r, h, *_: (r, 0, h)),
    )
    return pl.pallas_call(
        kernel,
        grid_spec=grid_spec,
        out_shape=jax.ShapeDtypeStruct((req_local, span_local, local_cols), jnp.bfloat16),
    )(*scalars, q_local, kv_parts, kv_parts, sink_keys, sink_values, parts_sum, parts_stats)


def shifted(x, axis_name, shift):
    count = lax.axis_size(axis_name)
    if shift % count == 0:
        return x
    return lax.ppermute(x, axis_name, [(a, (a + shift) % count) for a in range(count)])


def tp_sum(x):
    count = lax.axis_size("tp")
    assert count & (count - 1) == 0
    bit = 1
    while bit < count:
        x = x + lax.ppermute(x, "tp", [(a, a ^ bit) for a in range(count)])
        bit *= 2
    return x


def on_device(
    tokens,
    w_query,
    w_key,
    w_value,
    q_gain,
    k_gain,
    cache_keys,
    cache_values,
    sink_keys,
    sink_values,
    sink_pos,
    cache_len,
    span_len,
    window_len,
):
    req_local, span_local, model_width = tokens.shape
    local_cols = w_query.shape[1]
    seq_count = lax.axis_size("seq")
    seq_index = lax.axis_index("seq")
    token_rows = tokens.reshape(req_local * span_local, model_width)
    offsets = seq_index * span_local + jnp.arange(span_local, dtype=jnp.int32)
    positions = (cache_len[:, None] + offsets[None, :]).reshape(-1)
    wq_all = lax.all_gather(w_query, ("req", "seq"), axis=0, tiled=True)
    wkv_all = lax.all_gather(
        jnp.concatenate([w_key, w_value], axis=1), ("req", "seq"), axis=0, tiled=True
    )
    q_proj = jnp.dot(token_rows, wq_all, preferred_element_type=jnp.float32)
    q_squares = tp_sum(jnp.sum(q_proj * q_proj, axis=1))
    q_local = normalize_rotate(q_proj, q_squares, q_gain, positions, D, HEAD_DIM).reshape(
        req_local, span_local, local_cols
    )
    q_parts = jnp.stack([shifted(q_local, "seq", shift) for shift in range(seq_count)])
    c_sum, c_high, c_total = cache_attention(
        q_parts, cache_keys, cache_values, cache_len, window_len, seq_index
    )
    c_stats = jnp.concatenate([c_high, c_total], axis=-1)
    parts_sum = jnp.stack([shifted(c_sum[s], "seq", -s) for s in range(seq_count)])
    parts_stats = jnp.stack([shifted(c_stats[s], "seq", -s) for s in range(seq_count)])
    wkv_all, parts_sum, parts_stats = lax.optimization_barrier((wkv_all, parts_sum, parts_stats))
    kv_proj = jnp.dot(token_rows, wkv_all, preferred_element_type=jnp.float32)
    k_proj = kv_proj[:, :local_cols]
    k_squares = tp_sum(jnp.sum(k_proj * k_proj, axis=1))
    k_rot = normalize_rotate(k_proj, k_squares, k_gain, positions, D, HEAD_DIM)
    v_new = kv_proj[:, local_cols:].astype(jnp.bfloat16)
    kv_new = jnp.concatenate([k_rot, v_new], axis=1).reshape(req_local, span_local, 2 * local_cols)
    kv_parts = jnp.stack([shifted(kv_new, "seq", shift) for shift in range(seq_count)])
    scalars = (
        cache_len,
        window_len,
        jnp.reshape(seq_index, (1,)).astype(jnp.int32),
        span_len,
        sink_pos.reshape(-1),
    )
    return span_attention(
        q_local, kv_parts, sink_keys, sink_values, parts_sum, parts_stats, scalars
    )


def solution(mesh):
    placed = (
        P("req", "seq", None),
        P(("req", "seq"), "tp"),
        P(("req", "seq"), "tp"),
        P(("req", "seq"), "tp"),
        P("tp"),
        P("tp"),
        P("req", "seq", "tp"),
        P("req", "seq", "tp"),
        P("req", None, "tp"),
        P("req", None, "tp"),
        P("req", None),
        P("req"),
        P("req"),
        P("req"),
    )
    return jax.shard_map(
        on_device, mesh=mesh, in_specs=placed, out_specs=P("req", "seq", "tp"), check_vma=False
    )
```

```python
import functools

import jax
import jax.numpy as jnp
from jax import lax
from jax.experimental import pallas as pl
from jax.experimental.pallas import tpu as pltpu
from jax.sharding import PartitionSpec as P

D = 2048
HEAD_DIM = 128
WINDOW = 4096
SINKS = 4


rope_base = 500000.0
epsilon = 1e-06
lowest = -1e30


def rotate_heads(vectors, positions):
    half_dim = vectors.shape[-1] // 2
    powers = jnp.arange(half_dim, dtype=jnp.float32) * (2.0 / vectors.shape[-1])
    inverse = rope_base ** (-powers)
    angles = positions.astype(jnp.float32)[:, None] * inverse[None, :]
    cosine = jnp.cos(angles)[:, None, :]
    sine_part = jnp.sin(angles)[:, None, :]
    leading = vectors[..., :half_dim]
    trailing = vectors[..., half_dim:]
    return jnp.concatenate(
        [leading * cosine - trailing * sine_part, trailing * cosine + leading * sine_part], axis=-1
    )


def normalize_rotate(projected, squares, feature_gain, positions, model_width, head_size):
    factor = lax.rsqrt(squares / model_width + epsilon)
    normed = projected * factor[:, None] * feature_gain[None, :]
    shaped = normed.reshape(projected.shape[0], projected.shape[1] // head_size, head_size)
    return rotate_heads(shaped, positions).reshape(projected.shape).astype(jnp.bfloat16)


def cache_kernel(len_ref, win_ref, seq_ref, q_ref, ck_ref, cv_ref, o_ref, m_ref, l_ref, *, scaling):
    r = pl.program_id(0)
    length_now = len_ref[r]
    window_now = win_ref[r]
    seq_index = seq_ref[0]
    seq_count, _, span_local, _ = q_ref.shape
    slots = ck_ref.shape[1]
    keys = ck_ref[0]
    values = cv_ref[0]
    dims = (((1,), (1,)), ((), ()))
    row = lax.broadcasted_iota(jnp.int32, (span_local, slots), 0)
    slot = lax.broadcasted_iota(jnp.int32, (span_local, slots), 1) + seq_index * slots
    slot_pos = length_now - 1 - ((length_now - 1 - slot) & (WINDOW - 1))
    for shift in range(seq_count):
        owner = (seq_index - shift + seq_count) % seq_count
        scores = (
            lax.dot_general(q_ref[shift, 0], keys, dims, preferred_element_type=jnp.float32)
            * scaling
        )
        edge = length_now + owner * span_local + row - window_now
        allowed = (slot_pos >= 0) & (slot_pos > edge)
        highest = jnp.max(jnp.where(allowed, scores, lowest), axis=1, keepdims=True)
        weights = jnp.where(allowed, jnp.exp(scores - highest), 0.0)
        o_ref[shift, 0, 0] = jnp.dot(
            weights.astype(jnp.bfloat16), values, preferred_element_type=jnp.float32
        )
        m_ref[shift, 0, 0] = highest
        l_ref[shift, 0, 0] = jnp.sum(weights, axis=1, keepdims=True)


def cache_attention(q_parts, cache_keys, cache_values, cache_len, window_len, seq_index):
    seq_count, req_local, span_local, local_cols = q_parts.shape
    heads_local = local_cols // HEAD_DIM
    slot_local = cache_keys.shape[1]
    kernel = functools.partial(cache_kernel, scaling=HEAD_DIM ** (-0.5))
    part = (seq_count, 1, 1, span_local)
    grid_spec = pltpu.PrefetchScalarGridSpec(
        num_scalar_prefetch=3,
        grid=(req_local, heads_local),
        in_specs=[
            pl.BlockSpec((seq_count, 1, span_local, HEAD_DIM), lambda r, h, *_: (0, r, 0, h)),
            pl.BlockSpec((1, slot_local, HEAD_DIM), lambda r, h, *_: (r, 0, h)),
            pl.BlockSpec((1, slot_local, HEAD_DIM), lambda r, h, *_: (r, 0, h)),
        ],
        out_specs=[
            pl.BlockSpec(part + (HEAD_DIM,), lambda r, h, *_: (0, r, h, 0, 0)),
            pl.BlockSpec(part + (1,), lambda r, h, *_: (0, r, h, 0, 0)),
            pl.BlockSpec(part + (1,), lambda r, h, *_: (0, r, h, 0, 0)),
        ],
    )
    shape = (seq_count, req_local, heads_local, span_local)
    return pl.pallas_call(
        kernel,
        grid_spec=grid_spec,
        out_shape=[
            jax.ShapeDtypeStruct(shape + (HEAD_DIM,), jnp.float32),
            jax.ShapeDtypeStruct(shape + (1,), jnp.float32),
            jax.ShapeDtypeStruct(shape + (1,), jnp.float32),
        ],
    )(
        cache_len,
        window_len,
        jnp.reshape(seq_index, (1,)).astype(jnp.int32),
        q_parts,
        cache_keys,
        cache_values,
    )


def span_kernel(
    len_ref,
    win_ref,
    seq_ref,
    live_ref,
    sink_pos_ref,
    q_ref,
    nk_ref,
    nv_ref,
    sk_ref,
    sv_ref,
    ps_ref,
    pst_ref,
    out_ref,
    *,
    scaling,
):
    r = pl.program_id(0)
    length_now = len_ref[r]
    window_now = win_ref[r]
    seq_index = seq_ref[0]
    live_count = live_ref[r]
    seq_count, _, span_local, _ = nk_ref.shape
    queries = q_ref[0]
    dims = (((1,), (1,)), ((), ()))
    row = lax.broadcasted_iota(jnp.int32, (span_local, span_local), 0) + seq_index * span_local
    col = lax.broadcasted_iota(jnp.int32, (span_local, span_local), 1)
    span_scores, span_ok = [], []
    for shift in range(seq_count):
        owner = (seq_index - shift + seq_count) % seq_count
        span_scores.append(
            lax.dot_general(queries, nk_ref[shift, 0], dims, preferred_element_type=jnp.float32)
            * scaling
        )
        span_ok.append(owner * span_local + col <= row)
    query_f = queries.astype(jnp.float32)
    row_1 = lax.broadcasted_iota(jnp.int32, (span_local, 1), 0) + seq_index * span_local
    edge = length_now + row_1 - window_now
    sink_scores, sink_ok = [], []
    for sink in range(SINKS):
        key_f = sk_ref[0, sink : sink + 1, :].astype(jnp.float32)
        sink_scores.append(jnp.sum(query_f * key_f, axis=1, keepdims=True) * scaling)
        sink_ok.append(sink_pos_ref[r * SINKS + sink] <= edge)
    part_high = pst_ref[:, 0, 0, :, 0:1]
    part_total = pst_ref[:, 0, 0, :, 1:2]
    peak = jnp.max(part_high, axis=0)
    for scores, ok in zip(span_scores + sink_scores, span_ok + sink_ok):
        peak = jnp.maximum(peak, jnp.max(jnp.where(ok, scores, lowest), axis=1, keepdims=True))
    factor = jnp.exp(part_high - peak[None])
    denominator = jnp.sum(part_total * factor, axis=0)
    numerator = jnp.sum(ps_ref[:, 0, 0] * factor, axis=0)
    for shift in range(seq_count):
        weights = jnp.where(span_ok[shift], jnp.exp(span_scores[shift] - peak), 0.0)
        denominator = denominator + jnp.sum(weights, axis=1, keepdims=True)
        numerator = numerator + jnp.dot(
            weights.astype(jnp.bfloat16), nv_ref[shift, 0], preferred_element_type=jnp.float32
        )
    for sink in range(SINKS):
        weights = jnp.where(sink_ok[sink], jnp.exp(sink_scores[sink] - peak), 0.0)
        denominator = denominator + weights
        value_f = sv_ref[0, sink : sink + 1, :].astype(jnp.float32)
        numerator = numerator + weights.astype(jnp.bfloat16).astype(jnp.float32) * value_f
    live = row_1 < live_count
    safe = jnp.where(live, denominator, 1.0)
    out_ref[0] = jnp.where(live, numerator / safe, 0.0).astype(out_ref.dtype)


def span_attention(
    q_local, kv_parts, sink_keys, sink_values, parts_sum, parts_stats, scalars
):
    req_local, span_local, local_cols = q_local.shape
    seq_count = kv_parts.shape[0]
    heads_local = local_cols // HEAD_DIM
    kernel = functools.partial(span_kernel, scaling=HEAD_DIM ** (-0.5))
    part = (seq_count, 1, 1, span_local)
    grid_spec = pltpu.PrefetchScalarGridSpec(
        num_scalar_prefetch=5,
        grid=(req_local, heads_local),
        in_specs=[
            pl.BlockSpec((1, span_local, HEAD_DIM), lambda r, h, *_: (r, 0, h)),
            pl.BlockSpec((seq_count, 1, span_local, HEAD_DIM), lambda r, h, *_: (0, r, 0, h)),
            pl.BlockSpec(
                (seq_count, 1, span_local, HEAD_DIM),
                lambda r, h, *_: (0, r, 0, h + heads_local),
            ),
            pl.BlockSpec((1, SINKS, HEAD_DIM), lambda r, h, *_: (r, 0, h)),
            pl.BlockSpec((1, SINKS, HEAD_DIM), lambda r, h, *_: (r, 0, h)),
            pl.BlockSpec(part + (HEAD_DIM,), lambda r, h, *_: (0, r, h, 0, 0)),
            pl.BlockSpec(part + (2,), lambda r, h, *_: (0, r, h, 0, 0)),
        ],
        out_specs=pl.BlockSpec((1, span_local, HEAD_DIM), lambda r, h, *_: (r, 0, h)),
    )
    return pl.pallas_call(
        kernel,
        grid_spec=grid_spec,
        out_shape=jax.ShapeDtypeStruct((req_local, span_local, local_cols), jnp.bfloat16),
    )(*scalars, q_local, kv_parts, kv_parts, sink_keys, sink_values, parts_sum, parts_stats)


def shifted(x, axis_name, shift):
    count = lax.axis_size(axis_name)
    if shift % count == 0:
        return x
    return lax.ppermute(x, axis_name, [(a, (a + shift) % count) for a in range(count)])


def tp_sum(x):
    count = lax.axis_size("tp")
    assert count & (count - 1) == 0
    bit = 1
    while bit < count:
        x = x + lax.ppermute(x, "tp", [(a, a ^ bit) for a in range(count)])
        bit *= 2
    return x


def on_device(
    tokens,
    w_query,
    w_key,
    w_value,
    q_gain,
    k_gain,
    cache_keys,
    cache_values,
    sink_keys,
    sink_values,
    sink_pos,
    cache_len,
    span_len,
    window_len,
):
    req_local, span_local, model_width = tokens.shape
    local_cols = w_query.shape[1]
    seq_count = lax.axis_size("seq")
    seq_index = lax.axis_index("seq")
    token_rows = tokens.reshape(req_local * span_local, model_width)
    offsets = seq_index * span_local + jnp.arange(span_local, dtype=jnp.int32)
    positions = (cache_len[:, None] + offsets[None, :]).reshape(-1)
    wq_all = lax.all_gather(w_query, ("req", "seq"), axis=0, tiled=True)
    wkv_all = lax.all_gather(
        jnp.concatenate([w_key, w_value], axis=1), ("req", "seq"), axis=0, tiled=True
    )
    q_proj = jnp.dot(token_rows, wq_all, preferred_element_type=jnp.float32)
    q_squares = tp_sum(jnp.sum(q_proj * q_proj, axis=1))
    q_local = normalize_rotate(q_proj, q_squares, q_gain, positions, D, HEAD_DIM).reshape(
        req_local, span_local, local_cols
    )
    q_parts = jnp.stack([shifted(q_local, "seq", shift) for shift in range(seq_count)])
    c_sum, c_high, c_total = cache_attention(
        q_parts, cache_keys, cache_values, cache_len, window_len, seq_index
    )
    c_stats = jnp.concatenate([c_high, c_total], axis=-1)
    parts_sum = jnp.stack([shifted(c_sum[s], "seq", -s) for s in range(seq_count)])
    parts_stats = jnp.stack([shifted(c_stats[s], "seq", -s) for s in range(seq_count)])
    wkv_all, parts_sum, parts_stats = lax.optimization_barrier((wkv_all, parts_sum, parts_stats))
    kv_proj = jnp.dot(token_rows, wkv_all, preferred_element_type=jnp.float32)
    k_proj = kv_proj[:, :local_cols]
    k_squares = tp_sum(jnp.sum(k_proj * k_proj, axis=1))
    k_rot = normalize_rotate(k_proj, k_squares, k_gain, positions, D, HEAD_DIM)
    v_new = kv_proj[:, local_cols:].astype(jnp.bfloat16)
    kv_new = jnp.concatenate([k_rot, v_new], axis=1).reshape(req_local, span_local, 2 * local_cols)
    kv_parts = jnp.stack([shifted(kv_new, "seq", shift) for shift in range(seq_count)])
    scalars = (
        cache_len,
        window_len,
        jnp.reshape(seq_index, (1,)).astype(jnp.int32),
        span_len,
        sink_pos.reshape(-1),
    )
    return span_attention(
        q_local, kv_parts, sink_keys, sink_values, parts_sum, parts_stats, scalars
    )


def pair_cache_kernel(len_ref, win_ref, seq_ref, q_ref, ck_ref, cv_ref, o_ref, m_ref, l_ref, *, scaling):
    r = pl.program_id(0)
    length_now = len_ref[r]
    window_now = win_ref[r]
    seq_index = seq_ref[0]
    queries = q_ref[0]
    rows, slots = queries.shape[0], ck_ref.shape[1]
    dims = (((1,), (1,)), ((), ()))
    scores = (
        lax.dot_general(queries, ck_ref[0], dims, preferred_element_type=jnp.float32) * scaling
    )
    row = lax.broadcasted_iota(jnp.int32, (rows, slots), 0)
    slot = lax.broadcasted_iota(jnp.int32, (rows, slots), 1) + seq_index * slots
    edge = length_now + row - window_now
    slot_pos = length_now - 1 - ((length_now - 1 - slot) & (WINDOW - 1))
    allowed = (slot_pos >= 0) & (slot_pos > edge)
    highest = jnp.max(jnp.where(allowed, scores, lowest), axis=1, keepdims=True)
    weights = jnp.where(allowed, jnp.exp(scores - highest), 0.0)
    o_ref[0, 0] = jnp.dot(weights.astype(jnp.bfloat16), cv_ref[0], preferred_element_type=jnp.float32)
    m_ref[0, 0] = highest
    l_ref[0, 0] = jnp.sum(weights, axis=1, keepdims=True)


def pair_span_kernel(
    len_ref, win_ref, sink_pos_ref, seq_ref, q_ref, nk_ref, nv_ref, sk_ref, sv_ref, o_ref, m_ref, l_ref, *, scaling
):
    r = pl.program_id(0)
    length_now = len_ref[r]
    window_now = win_ref[r]
    queries = q_ref[0]
    rows = queries.shape[0]
    dims = (((1,), (1,)), ((), ()))
    scores = (
        lax.dot_general(queries, nk_ref[0], dims, preferred_element_type=jnp.float32) * scaling
    )
    row = lax.broadcasted_iota(jnp.int32, scores.shape, 0)
    key = lax.broadcasted_iota(jnp.int32, scores.shape, 1)
    allowed = key <= row
    query_f = queries.astype(jnp.float32)
    row_1 = lax.broadcasted_iota(jnp.int32, (rows, 1), 0)
    edge = length_now + row_1 - window_now
    sink_scores, sink_ok = [], []
    for sink in range(SINKS):
        key_f = sk_ref[0, sink : sink + 1, :].astype(jnp.float32)
        sink_scores.append(jnp.sum(query_f * key_f, axis=1, keepdims=True) * scaling)
        sink_ok.append(sink_pos_ref[r * SINKS + sink] <= edge)
    highest = jnp.max(jnp.where(allowed, scores, lowest), axis=1, keepdims=True)
    for part, ok in zip(sink_scores, sink_ok):
        highest = jnp.maximum(highest, jnp.where(ok, part, lowest))
    weights = jnp.where(allowed, jnp.exp(scores - highest), 0.0)
    totals = jnp.sum(weights, axis=1, keepdims=True)
    summed = jnp.dot(weights.astype(jnp.bfloat16), nv_ref[0], preferred_element_type=jnp.float32)
    for sink in range(SINKS):
        sink_w = jnp.where(sink_ok[sink], jnp.exp(sink_scores[sink] - highest), 0.0)
        totals = totals + sink_w
        value_f = sv_ref[0, sink : sink + 1, :].astype(jnp.float32)
        summed = summed + sink_w.astype(jnp.bfloat16).astype(jnp.float32) * value_f
    o_ref[0, 0] = summed
    m_ref[0, 0] = highest
    l_ref[0, 0] = totals


def pair_partials(kernel, scalars, q_spec_index, operands, in_specs, req_local, heads, rows):
    grid_spec = pltpu.PrefetchScalarGridSpec(
        num_scalar_prefetch=len(scalars),
        grid=(req_local, heads),
        in_specs=in_specs,
        out_specs=[
            pl.BlockSpec((1, 1, rows, HEAD_DIM), lambda r, h, *_: (r, h, 0, 0)),
            pl.BlockSpec((1, 1, rows, 1), lambda r, h, *_: (r, h, 0, 0)),
            pl.BlockSpec((1, 1, rows, 1), lambda r, h, *_: (r, h, 0, 0)),
        ],
    )
    shape = (req_local, heads, rows)
    return pl.pallas_call(
        functools.partial(kernel, scaling=HEAD_DIM ** (-0.5)),
        grid_spec=grid_spec,
        out_shape=[
            jax.ShapeDtypeStruct(shape + (HEAD_DIM,), jnp.float32),
            jax.ShapeDtypeStruct(shape + (1,), jnp.float32),
            jax.ShapeDtypeStruct(shape + (1,), jnp.float32),
        ],
    )(*scalars, *operands)


def merge_parts(first, second):
    s1, m1, l1 = first
    s2, m2, l2 = second
    peak = jnp.maximum(m1, m2)
    f1 = jnp.exp(m1 - peak)
    f2 = jnp.exp(m2 - peak)
    return (s1 * f1 + s2 * f2, peak, l1 * f1 + l2 * f2)


def swap_seq(x):
    return lax.ppermute(x, "seq", [(0, 1), (1, 0)])


def on_device_pair(
    tokens,
    w_query,
    w_key,
    w_value,
    q_gain,
    k_gain,
    cache_keys,
    cache_values,
    sink_keys,
    sink_values,
    sink_pos,
    cache_len,
    span_len,
    window_len,
):
    req_local, span_local, model_width = tokens.shape
    local_cols = w_query.shape[1]
    half = local_cols // 2
    heads_local = local_cols // HEAD_DIM
    heads_half = heads_local // 2
    seq_index = lax.axis_index("seq")
    first = seq_index == 0
    span_total = 2 * span_local
    slot_local = cache_keys.shape[1]
    weights = (w_query, w_key, w_value)
    mine = jnp.concatenate(
        [lax.dynamic_slice_in_dim(w, seq_index * half, half, axis=1) for w in weights], axis=1
    )
    other = jnp.concatenate(
        [lax.dynamic_slice_in_dim(w, (1 - seq_index) * half, half, axis=1) for w in weights], axis=1
    )
    got = swap_seq(other)
    pair_rows = jnp.where(first, jnp.concatenate([mine, got], 0), jnp.concatenate([got, mine], 0))
    w_all = lax.all_gather(pair_rows, "req", axis=0, tiled=True)
    tokens_other = swap_seq(tokens)
    tokens_all = jnp.where(
        first,
        jnp.concatenate([tokens, tokens_other], axis=1),
        jnp.concatenate([tokens_other, tokens], axis=1),
    )
    token_rows = tokens_all.reshape(req_local * span_total, model_width)
    proj = jnp.dot(token_rows, w_all, preferred_element_type=jnp.float32)
    q_proj = proj[:, :half]
    k_proj = proj[:, half : 2 * half]
    v_proj = proj[:, 2 * half :]
    squares = jnp.stack([jnp.sum(q_proj * q_proj, axis=1), jnp.sum(k_proj * k_proj, axis=1)])
    squares = tp_sum(squares)
    squares = squares + swap_seq(squares)
    offsets = jnp.arange(span_total, dtype=jnp.int32)
    positions = (cache_len[:, None] + offsets[None, :]).reshape(-1)
    q_gain_half = lax.dynamic_slice_in_dim(q_gain, seq_index * half, half)
    k_gain_half = lax.dynamic_slice_in_dim(k_gain, seq_index * half, half)
    q_half = normalize_rotate(q_proj, squares[0], q_gain_half, positions, D, HEAD_DIM).reshape(
        req_local, span_total, half
    )
    k_half = normalize_rotate(k_proj, squares[1], k_gain_half, positions, D, HEAD_DIM).reshape(
        req_local, span_total, half
    )
    v_half = v_proj.astype(jnp.bfloat16).reshape(req_local, span_total, half)
    q_other = swap_seq(q_half)
    q_full = jnp.where(
        first, jnp.concatenate([q_half, q_other], -1), jnp.concatenate([q_other, q_half], -1)
    )
    seq_arr = jnp.reshape(seq_index, (1,)).astype(jnp.int32)
    head_block = lambda r, h, *_: (r, 0, h)
    cache_part = pair_partials(
        pair_cache_kernel,
        (cache_len, window_len, seq_arr),
        None,
        (q_full, cache_keys, cache_values),
        [
            pl.BlockSpec((1, span_total, HEAD_DIM), head_block),
            pl.BlockSpec((1, slot_local, HEAD_DIM), head_block),
            pl.BlockSpec((1, slot_local, HEAD_DIM), head_block),
        ],
        req_local,
        heads_local,
        span_total,
    )
    sink_block = lambda r, h, len_ref, win_ref, pos_ref, seq_ref: (r, 0, h + seq_ref[0] * heads_half)
    span_part = pair_partials(
        pair_span_kernel,
        (cache_len, window_len, sink_pos.reshape(-1), seq_arr),
        None,
        (q_half, k_half, v_half, sink_keys, sink_values),
        [
            pl.BlockSpec((1, span_total, HEAD_DIM), head_block),
            pl.BlockSpec((1, span_total, HEAD_DIM), head_block),
            pl.BlockSpec((1, span_total, HEAD_DIM), head_block),
            pl.BlockSpec((1, SINKS, HEAD_DIM), sink_block),
            pl.BlockSpec((1, SINKS, HEAD_DIM), sink_block),
        ],
        req_local,
        heads_half,
        span_total,
    )
    empty = (
        jnp.zeros_like(cache_part[0]),
        jnp.full_like(cache_part[1], lowest),
        jnp.zeros_like(cache_part[2]),
    )
    span_wide = tuple(
        lax.dynamic_update_slice_in_dim(e, p, seq_index * heads_half, axis=1)
        for e, p in zip(empty, span_part)
    )
    merged = merge_parts(cache_part, span_wide)
    own_rows = tuple(
        lax.dynamic_slice_in_dim(x, seq_index * span_local, span_local, axis=2) for x in merged
    )
    far_rows = tuple(
        lax.dynamic_slice_in_dim(x, (1 - seq_index) * span_local, span_local, axis=2)
        for x in merged
    )
    got_sum = swap_seq(far_rows[0])
    got_stats = swap_seq(jnp.concatenate([far_rows[1], far_rows[2]], axis=-1))
    total_sum, _, total = merge_parts(own_rows, (got_sum, got_stats[..., 0:1], got_stats[..., 1:2]))
    own_offsets = seq_index * span_local + jnp.arange(span_local, dtype=jnp.int32)
    live_rows = (own_offsets[None, :] < span_len[:, None])[:, None, :, None]
    safe_total = jnp.where(live_rows, total, 1.0)
    mixed = jnp.where(live_rows, total_sum / safe_total, 0.0)
    return (
        mixed.transpose(0, 2, 1, 3).reshape(req_local, span_local, local_cols).astype(jnp.bfloat16)
    )


def solution(mesh):
    placed = (
        P("req", "seq", None),
        P(("req", "seq"), "tp"),
        P(("req", "seq"), "tp"),
        P(("req", "seq"), "tp"),
        P("tp"),
        P("tp"),
        P("req", "seq", "tp"),
        P("req", "seq", "tp"),
        P("req", None, "tp"),
        P("req", None, "tp"),
        P("req", None),
        P("req"),
        P("req"),
        P("req"),
    )
    body = on_device_pair if mesh.shape["seq"] == 2 else on_device
    return jax.shard_map(
        body, mesh=mesh, in_specs=placed, out_specs=P("req", "seq", "tp"), check_vma=False
    )
```

```python
import functools

import jax
import jax.numpy as jnp
from jax import lax
from jax.experimental import pallas as pl
from jax.experimental.pallas import tpu as pltpu
from jax.sharding import PartitionSpec as P

D = 2048
HEAD_DIM = 128
WINDOW = 4096
SINKS = 4


rope_base = 500000.0
epsilon = 1e-06
lowest = -1e30


def rotate_heads(vectors, positions):
    half_dim = vectors.shape[-1] // 2
    powers = jnp.arange(half_dim, dtype=jnp.float32) * (2.0 / vectors.shape[-1])
    inverse = rope_base ** (-powers)
    angles = positions.astype(jnp.float32)[:, None] * inverse[None, :]
    cosine = jnp.cos(angles)[:, None, :]
    sine_part = jnp.sin(angles)[:, None, :]
    leading = vectors[..., :half_dim]
    trailing = vectors[..., half_dim:]
    return jnp.concatenate(
        [leading * cosine - trailing * sine_part, trailing * cosine + leading * sine_part], axis=-1
    )


def normalize_rotate(projected, squares, feature_gain, positions, model_width, head_size):
    factor = lax.rsqrt(squares / model_width + epsilon)
    normed = projected * factor[:, None] * feature_gain[None, :]
    shaped = normed.reshape(projected.shape[0], projected.shape[1] // head_size, head_size)
    return rotate_heads(shaped, positions).reshape(projected.shape).astype(jnp.bfloat16)


def cache_kernel(len_ref, win_ref, seq_ref, q_ref, ck_ref, cv_ref, o_ref, m_ref, l_ref, *, scaling):
    r = pl.program_id(0)
    length_now = len_ref[r]
    window_now = win_ref[r]
    seq_index = seq_ref[0]
    seq_count, _, span_local, _ = q_ref.shape
    slots = ck_ref.shape[1]
    keys = ck_ref[0]
    values = cv_ref[0]
    dims = (((1,), (1,)), ((), ()))
    row = lax.broadcasted_iota(jnp.int32, (span_local, slots), 0)
    slot = lax.broadcasted_iota(jnp.int32, (span_local, slots), 1) + seq_index * slots
    slot_pos = length_now - 1 - ((length_now - 1 - slot) & (WINDOW - 1))
    for shift in range(seq_count):
        owner = (seq_index - shift + seq_count) % seq_count
        scores = (
            lax.dot_general(q_ref[shift, 0], keys, dims, preferred_element_type=jnp.float32)
            * scaling
        )
        edge = length_now + owner * span_local + row - window_now
        allowed = (slot_pos >= 0) & (slot_pos > edge)
        highest = jnp.max(jnp.where(allowed, scores, lowest), axis=1, keepdims=True)
        weights = jnp.where(allowed, jnp.exp(scores - highest), 0.0)
        o_ref[shift, 0, 0] = jnp.dot(
            weights.astype(jnp.bfloat16), values, preferred_element_type=jnp.float32
        )
        m_ref[shift, 0, 0] = highest
        l_ref[shift, 0, 0] = jnp.sum(weights, axis=1, keepdims=True)


def cache_attention(q_parts, cache_keys, cache_values, cache_len, window_len, seq_index):
    seq_count, req_local, span_local, local_cols = q_parts.shape
    heads_local = local_cols // HEAD_DIM
    slot_local = cache_keys.shape[1]
    kernel = functools.partial(cache_kernel, scaling=HEAD_DIM ** (-0.5))
    part = (seq_count, 1, 1, span_local)
    grid_spec = pltpu.PrefetchScalarGridSpec(
        num_scalar_prefetch=3,
        grid=(req_local, heads_local),
        in_specs=[
            pl.BlockSpec((seq_count, 1, span_local, HEAD_DIM), lambda r, h, *_: (0, r, 0, h)),
            pl.BlockSpec((1, slot_local, HEAD_DIM), lambda r, h, *_: (r, 0, h)),
            pl.BlockSpec((1, slot_local, HEAD_DIM), lambda r, h, *_: (r, 0, h)),
        ],
        out_specs=[
            pl.BlockSpec(part + (HEAD_DIM,), lambda r, h, *_: (0, r, h, 0, 0)),
            pl.BlockSpec(part + (1,), lambda r, h, *_: (0, r, h, 0, 0)),
            pl.BlockSpec(part + (1,), lambda r, h, *_: (0, r, h, 0, 0)),
        ],
    )
    shape = (seq_count, req_local, heads_local, span_local)
    return pl.pallas_call(
        kernel,
        grid_spec=grid_spec,
        out_shape=[
            jax.ShapeDtypeStruct(shape + (HEAD_DIM,), jnp.float32),
            jax.ShapeDtypeStruct(shape + (1,), jnp.float32),
            jax.ShapeDtypeStruct(shape + (1,), jnp.float32),
        ],
    )(
        cache_len,
        window_len,
        jnp.reshape(seq_index, (1,)).astype(jnp.int32),
        q_parts,
        cache_keys,
        cache_values,
    )


def span_kernel(
    len_ref,
    win_ref,
    seq_ref,
    live_ref,
    sink_pos_ref,
    q_ref,
    nk_ref,
    nv_ref,
    sk_ref,
    sv_ref,
    ps_ref,
    pst_ref,
    out_ref,
    *,
    scaling,
):
    r = pl.program_id(0)
    length_now = len_ref[r]
    window_now = win_ref[r]
    seq_index = seq_ref[0]
    live_count = live_ref[r]
    seq_count, _, span_local, _ = nk_ref.shape
    queries = q_ref[0]
    dims = (((1,), (1,)), ((), ()))
    row = lax.broadcasted_iota(jnp.int32, (span_local, span_local), 0) + seq_index * span_local
    col = lax.broadcasted_iota(jnp.int32, (span_local, span_local), 1)
    span_scores, span_ok = [], []
    for shift in range(seq_count):
        owner = (seq_index - shift + seq_count) % seq_count
        span_scores.append(
            lax.dot_general(queries, nk_ref[shift, 0], dims, preferred_element_type=jnp.float32)
            * scaling
        )
        span_ok.append(owner * span_local + col <= row)
    query_f = queries.astype(jnp.float32)
    row_1 = lax.broadcasted_iota(jnp.int32, (span_local, 1), 0) + seq_index * span_local
    edge = length_now + row_1 - window_now
    sink_scores, sink_ok = [], []
    for sink in range(SINKS):
        key_f = sk_ref[0, sink : sink + 1, :].astype(jnp.float32)
        sink_scores.append(jnp.sum(query_f * key_f, axis=1, keepdims=True) * scaling)
        sink_ok.append(sink_pos_ref[r * SINKS + sink] <= edge)
    part_high = pst_ref[:, 0, 0, :, 0:1]
    part_total = pst_ref[:, 0, 0, :, 1:2]
    peak = jnp.max(part_high, axis=0)
    for scores, ok in zip(span_scores + sink_scores, span_ok + sink_ok):
        peak = jnp.maximum(peak, jnp.max(jnp.where(ok, scores, lowest), axis=1, keepdims=True))
    factor = jnp.exp(part_high - peak[None])
    denominator = jnp.sum(part_total * factor, axis=0)
    numerator = jnp.sum(ps_ref[:, 0, 0] * factor, axis=0)
    for shift in range(seq_count):
        weights = jnp.where(span_ok[shift], jnp.exp(span_scores[shift] - peak), 0.0)
        denominator = denominator + jnp.sum(weights, axis=1, keepdims=True)
        numerator = numerator + jnp.dot(
            weights.astype(jnp.bfloat16), nv_ref[shift, 0], preferred_element_type=jnp.float32
        )
    for sink in range(SINKS):
        weights = jnp.where(sink_ok[sink], jnp.exp(sink_scores[sink] - peak), 0.0)
        denominator = denominator + weights
        value_f = sv_ref[0, sink : sink + 1, :].astype(jnp.float32)
        numerator = numerator + weights.astype(jnp.bfloat16).astype(jnp.float32) * value_f
    live = row_1 < live_count
    safe = jnp.where(live, denominator, 1.0)
    out_ref[0] = jnp.where(live, numerator / safe, 0.0).astype(out_ref.dtype)


def span_attention(
    q_local, kv_parts, sink_keys, sink_values, parts_sum, parts_stats, scalars
):
    req_local, span_local, local_cols = q_local.shape
    seq_count = kv_parts.shape[0]
    heads_local = local_cols // HEAD_DIM
    kernel = functools.partial(span_kernel, scaling=HEAD_DIM ** (-0.5))
    part = (seq_count, 1, 1, span_local)
    grid_spec = pltpu.PrefetchScalarGridSpec(
        num_scalar_prefetch=5,
        grid=(req_local, heads_local),
        in_specs=[
            pl.BlockSpec((1, span_local, HEAD_DIM), lambda r, h, *_: (r, 0, h)),
            pl.BlockSpec((seq_count, 1, span_local, HEAD_DIM), lambda r, h, *_: (0, r, 0, h)),
            pl.BlockSpec(
                (seq_count, 1, span_local, HEAD_DIM),
                lambda r, h, *_: (0, r, 0, h + heads_local),
            ),
            pl.BlockSpec((1, SINKS, HEAD_DIM), lambda r, h, *_: (r, 0, h)),
            pl.BlockSpec((1, SINKS, HEAD_DIM), lambda r, h, *_: (r, 0, h)),
            pl.BlockSpec(part + (HEAD_DIM,), lambda r, h, *_: (0, r, h, 0, 0)),
            pl.BlockSpec(part + (2,), lambda r, h, *_: (0, r, h, 0, 0)),
        ],
        out_specs=pl.BlockSpec((1, span_local, HEAD_DIM), lambda r, h, *_: (r, 0, h)),
    )
    return pl.pallas_call(
        kernel,
        grid_spec=grid_spec,
        out_shape=jax.ShapeDtypeStruct((req_local, span_local, local_cols), jnp.bfloat16),
    )(*scalars, q_local, kv_parts, kv_parts, sink_keys, sink_values, parts_sum, parts_stats)


def shifted(x, axis_name, shift):
    count = lax.axis_size(axis_name)
    if shift % count == 0:
        return x
    return lax.ppermute(x, axis_name, [(a, (a + shift) % count) for a in range(count)])


def tp_sum(x):
    count = lax.axis_size("tp")
    assert count & (count - 1) == 0
    bit = 1
    while bit < count:
        x = x + lax.ppermute(x, "tp", [(a, a ^ bit) for a in range(count)])
        bit *= 2
    return x


def on_device(
    tokens,
    w_query,
    w_key,
    w_value,
    q_gain,
    k_gain,
    cache_keys,
    cache_values,
    sink_keys,
    sink_values,
    sink_pos,
    cache_len,
    span_len,
    window_len,
):
    req_local, span_local, model_width = tokens.shape
    local_cols = w_query.shape[1]
    seq_count = lax.axis_size("seq")
    seq_index = lax.axis_index("seq")
    token_rows = tokens.reshape(req_local * span_local, model_width)
    offsets = seq_index * span_local + jnp.arange(span_local, dtype=jnp.int32)
    positions = (cache_len[:, None] + offsets[None, :]).reshape(-1)
    wq_all = lax.all_gather(w_query, ("req", "seq"), axis=0, tiled=True)
    wkv_all = lax.all_gather(
        jnp.concatenate([w_key, w_value], axis=1), ("req", "seq"), axis=0, tiled=True
    )
    q_proj = jnp.dot(token_rows, wq_all, preferred_element_type=jnp.float32)
    q_squares = tp_sum(jnp.sum(q_proj * q_proj, axis=1))
    q_local = normalize_rotate(q_proj, q_squares, q_gain, positions, D, HEAD_DIM).reshape(
        req_local, span_local, local_cols
    )
    q_parts = jnp.stack([shifted(q_local, "seq", shift) for shift in range(seq_count)])
    c_sum, c_high, c_total = cache_attention(
        q_parts, cache_keys, cache_values, cache_len, window_len, seq_index
    )
    c_stats = jnp.concatenate([c_high, c_total], axis=-1)
    parts_sum = jnp.stack([shifted(c_sum[s], "seq", -s) for s in range(seq_count)])
    parts_stats = jnp.stack([shifted(c_stats[s], "seq", -s) for s in range(seq_count)])
    wkv_all, parts_sum, parts_stats = lax.optimization_barrier((wkv_all, parts_sum, parts_stats))
    kv_proj = jnp.dot(token_rows, wkv_all, preferred_element_type=jnp.float32)
    k_proj = kv_proj[:, :local_cols]
    k_squares = tp_sum(jnp.sum(k_proj * k_proj, axis=1))
    k_rot = normalize_rotate(k_proj, k_squares, k_gain, positions, D, HEAD_DIM)
    v_new = kv_proj[:, local_cols:].astype(jnp.bfloat16)
    kv_new = jnp.concatenate([k_rot, v_new], axis=1).reshape(req_local, span_local, 2 * local_cols)
    kv_parts = jnp.stack([shifted(kv_new, "seq", shift) for shift in range(seq_count)])
    scalars = (
        cache_len,
        window_len,
        jnp.reshape(seq_index, (1,)).astype(jnp.int32),
        span_len,
        sink_pos.reshape(-1),
    )
    return span_attention(
        q_local, kv_parts, sink_keys, sink_values, parts_sum, parts_stats, scalars
    )


def pair_cache_kernel(
    len_ref, win_ref, seq_ref, first_ref, q_ref, ck_ref, cv_ref, o_ref, m_ref, l_ref, *, scaling
):
    r = pl.program_id(0)
    length_now = len_ref[r] + first_ref[0]
    window_now = win_ref[r]
    seq_index = seq_ref[0]
    rows, slots = q_ref.shape[1], ck_ref.shape[1]
    heads = q_ref.shape[2] // HEAD_DIM
    dims = (((1,), (1,)), ((), ()))
    row = lax.broadcasted_iota(jnp.int32, (rows, slots), 0)
    slot = lax.broadcasted_iota(jnp.int32, (rows, slots), 1) + seq_index * slots
    edge = length_now + row - window_now
    slot_pos = length_now - 1 - ((length_now - 1 - slot) & (WINDOW - 1))
    allowed = (slot_pos >= 0) & (slot_pos > edge)
    bias = jnp.where(allowed, 0.0, lowest)
    for h in range(heads):
        cols = slice(h * HEAD_DIM, (h + 1) * HEAD_DIM)
        scores = (
            lax.dot_general(q_ref[0, :, cols], ck_ref[0, :, cols], dims, preferred_element_type=jnp.float32)
            * scaling
            + bias
        )
        highest = jnp.max(scores, axis=1, keepdims=True)
        weights = jnp.exp(scores - highest)
        some = highest > lowest
        o_ref[0, h] = jnp.where(
            some,
            jnp.dot(weights.astype(jnp.bfloat16), cv_ref[0, :, cols], preferred_element_type=jnp.float32),
            0.0,
        )
        m_ref[0, h] = highest
        l_ref[0, h] = jnp.where(some, jnp.sum(weights, axis=1, keepdims=True), 0.0)


def pair_span_kernel(
    len_ref, win_ref, sink_pos_ref, seq_ref, q_ref, nk_ref, nv_ref, sk_ref, sv_ref, o_ref, m_ref, l_ref, *, scaling
):
    r = pl.program_id(0)
    length_now = len_ref[r]
    window_now = win_ref[r]
    rows = q_ref.shape[1]
    heads = q_ref.shape[2] // HEAD_DIM
    dims = (((1,), (1,)), ((), ()))
    row = lax.broadcasted_iota(jnp.int32, (rows, rows), 0)
    key = lax.broadcasted_iota(jnp.int32, (rows, rows), 1)
    allowed = key <= row
    row_1 = lax.broadcasted_iota(jnp.int32, (rows, 1), 0)
    edge = length_now + row_1 - window_now
    sink_ok = [sink_pos_ref[r * SINKS + sink] <= edge for sink in range(SINKS)]
    for h in range(heads):
        cols = slice(h * HEAD_DIM, (h + 1) * HEAD_DIM)
        queries = q_ref[0, :, cols]
        scores = (
            lax.dot_general(queries, nk_ref[0, :, cols], dims, preferred_element_type=jnp.float32)
            * scaling
        )
        query_f = queries.astype(jnp.float32)
        sink_scores = []
        for sink in range(SINKS):
            key_f = sk_ref[0, sink : sink + 1, cols].astype(jnp.float32)
            sink_scores.append(jnp.sum(query_f * key_f, axis=1, keepdims=True) * scaling)
        highest = jnp.max(jnp.where(allowed, scores, lowest), axis=1, keepdims=True)
        for part, ok in zip(sink_scores, sink_ok):
            highest = jnp.maximum(highest, jnp.where(ok, part, lowest))
        weights = jnp.where(allowed, jnp.exp(scores - highest), 0.0)
        totals = jnp.sum(weights, axis=1, keepdims=True)
        summed = jnp.dot(
            weights.astype(jnp.bfloat16), nv_ref[0, :, cols], preferred_element_type=jnp.float32
        )
        for sink in range(SINKS):
            sink_w = jnp.where(sink_ok[sink], jnp.exp(sink_scores[sink] - highest), 0.0)
            totals = totals + sink_w
            value_f = sv_ref[0, sink : sink + 1, cols].astype(jnp.float32)
            summed = summed + sink_w.astype(jnp.bfloat16).astype(jnp.float32) * value_f
        o_ref[0, h] = summed
        m_ref[0, h] = highest
        l_ref[0, h] = totals


def merged_cache_kernel(
    len_ref, win_ref, seq_ref, first_ref, owner_ref, qa_ref, qb_ref, ck_ref, cv_ref, ss_ref, sm_ref,
    sl_ref, o_ref, st_ref, *, scaling, normalize
):
    r = pl.program_id(0)
    length_now = len_ref[r] + first_ref[0]
    window_now = win_ref[r]
    seq_index = seq_ref[0]
    rows, slots = qa_ref.shape[1], ck_ref.shape[1]
    heads_half = ss_ref.shape[1]
    heads = 2 * heads_half
    dims = (((1,), (1,)), ((), ()))
    row = lax.broadcasted_iota(jnp.int32, (rows, slots), 0)
    slot = lax.broadcasted_iota(jnp.int32, (rows, slots), 1) + seq_index * slots
    edge = length_now + row - window_now
    cached = len_ref[r]
    slot_pos = cached - 1 - ((cached - 1 - slot) & (WINDOW - 1))
    allowed = (slot_pos >= 0) & (slot_pos > edge)
    bias = jnp.where(allowed, 0.0, lowest)
    for h in range(heads):
        cols = slice(h * HEAD_DIM, (h + 1) * HEAD_DIM)
        j = h % heads_half
        local = slice(j * HEAD_DIM, (j + 1) * HEAD_DIM)
        here = (h // heads_half) == seq_index
        queries = jnp.where(here, qa_ref[0, :, local], qb_ref[0, :, local])
        scores = (
            lax.dot_general(queries, ck_ref[0, :, cols], dims, preferred_element_type=jnp.float32)
            * scaling
            + bias
        )
        highest = jnp.max(scores, axis=1, keepdims=True)
        weights = jnp.exp(scores - highest)
        some = highest > lowest
        summed = jnp.where(
            some,
            jnp.dot(weights.astype(jnp.bfloat16), cv_ref[0, :, cols], preferred_element_type=jnp.float32),
            0.0,
        )
        totals = jnp.where(some, jnp.sum(weights, axis=1, keepdims=True), 0.0)
        span_high = sm_ref[0, j]
        peak = jnp.maximum(highest, span_high)
        f_cache = jnp.exp(highest - peak)
        f_span = jnp.exp(span_high - peak)
        summed = jnp.where(here, summed * f_cache + ss_ref[0, j] * f_span, summed)
        totals = jnp.where(here, totals * f_cache + sl_ref[0, j] * f_span, totals)
        highest = jnp.where(here, peak, highest)
        if normalize:
            summed = summed / jnp.where(totals > 0, totals, 1.0)
        o_ref[0, h] = summed.astype(o_ref.dtype)
        st_ref[0, h, :, 0:1] = highest
        st_ref[0, h, :, 1:2] = totals


def pair_partials(kernel, scalars, q_spec_index, operands, in_specs, req_local, heads, rows):
    grid_spec = pltpu.PrefetchScalarGridSpec(
        num_scalar_prefetch=len(scalars),
        grid=(req_local,),
        in_specs=in_specs,
        out_specs=[
            pl.BlockSpec((1, heads, rows, HEAD_DIM), lambda r, *_: (r, 0, 0, 0)),
            pl.BlockSpec((1, heads, rows, 1), lambda r, *_: (r, 0, 0, 0)),
            pl.BlockSpec((1, heads, rows, 1), lambda r, *_: (r, 0, 0, 0)),
        ],
    )
    shape = (req_local, heads, rows)
    return pl.pallas_call(
        functools.partial(kernel, scaling=HEAD_DIM ** (-0.5)),
        grid_spec=grid_spec,
        out_shape=[
            jax.ShapeDtypeStruct(shape + (HEAD_DIM,), jnp.float32),
            jax.ShapeDtypeStruct(shape + (1,), jnp.float32),
            jax.ShapeDtypeStruct(shape + (1,), jnp.float32),
        ],
    )(*scalars, *operands)


def merge_parts(first, second):
    s1, m1, l1 = first
    s2, m2, l2 = second
    peak = jnp.maximum(m1, m2)
    f1 = jnp.exp(m1 - peak)
    f2 = jnp.exp(m2 - peak)
    return (s1 * f1 + s2 * f2, peak, l1 * f1 + l2 * f2)


def swap_seq(x):
    return lax.ppermute(x, "seq", [(0, 1), (1, 0)])


def on_device_pair(
    tokens,
    w_query,
    w_key,
    w_value,
    q_gain,
    k_gain,
    cache_keys,
    cache_values,
    sink_keys,
    sink_values,
    sink_pos,
    cache_len,
    span_len,
    window_len,
):
    req_local, span_local, model_width = tokens.shape
    local_cols = w_query.shape[1]
    half = local_cols // 2
    heads_local = local_cols // HEAD_DIM
    heads_half = heads_local // 2
    seq_index = lax.axis_index("seq")
    first = seq_index == 0
    span_total = 2 * span_local
    slot_local = cache_keys.shape[1]
    weights = (w_query, w_key, w_value)
    other = jnp.concatenate(
        [jnp.where(first, w[:, half:], w[:, :half]) for w in weights], axis=1
    )
    got = swap_seq(other)
    mine = jnp.concatenate(
        [jnp.where(first, w[:, :half], w[:, half:]) for w in weights], axis=1
    )
    w_all = lax.all_gather(jnp.concatenate([mine, got], 0), "req", axis=0, tiled=True)
    tokens_other = swap_seq(tokens)
    tokens_all = jnp.where(
        first,
        jnp.concatenate([tokens, tokens_other], axis=1),
        jnp.concatenate([tokens_other, tokens], axis=1),
    )
    row_block = w_query.shape[0]
    blocks = tokens_all.reshape(req_local, span_total, model_width // (2 * row_block), 2, row_block)
    tokens_all = jnp.where(first, blocks, blocks[:, :, :, ::-1, :]).reshape(tokens_all.shape)
    token_rows = tokens_all.reshape(req_local * span_total, model_width)
    proj = jnp.dot(token_rows, w_all, preferred_element_type=jnp.float32)
    q_proj = proj[:, :half]
    k_proj = proj[:, half : 2 * half]
    v_proj = proj[:, 2 * half :]
    squares = jnp.stack([jnp.sum(q_proj * q_proj, axis=1), jnp.sum(k_proj * k_proj, axis=1)])
    squares = tp_sum(squares)
    squares = squares + swap_seq(squares)
    offsets = jnp.arange(span_total, dtype=jnp.int32)
    positions = (cache_len[:, None] + offsets[None, :]).reshape(-1)
    q_gain_half = lax.dynamic_slice_in_dim(q_gain, seq_index * half, half)
    k_gain_half = lax.dynamic_slice_in_dim(k_gain, seq_index * half, half)
    q_half = normalize_rotate(q_proj, squares[0], q_gain_half, positions, D, HEAD_DIM).reshape(
        req_local, span_total, half
    )
    k_half = normalize_rotate(k_proj, squares[1], k_gain_half, positions, D, HEAD_DIM).reshape(
        req_local, span_total, half
    )
    v_half = v_proj.astype(jnp.bfloat16).reshape(req_local, span_total, half)
    q_other = swap_seq(q_half)
    q_full = jnp.where(
        first, jnp.concatenate([q_half, q_other], -1), jnp.concatenate([q_other, q_half], -1)
    )
    seq_arr = jnp.reshape(seq_index, (1,)).astype(jnp.int32)
    head_block = lambda r, *_: (r, 0, 0)
    sink_block = lambda r, len_ref, win_ref, pos_ref, seq_ref: (r, 0, seq_ref[0])
    span_part = pair_partials(
        pair_span_kernel,
        (cache_len, window_len, sink_pos.reshape(-1), seq_arr),
        None,
        (q_half, k_half, v_half, sink_keys, sink_values),
        [
            pl.BlockSpec((1, span_total, half), head_block),
            pl.BlockSpec((1, span_total, half), head_block),
            pl.BlockSpec((1, span_total, half), head_block),
            pl.BlockSpec((1, SINKS, half), sink_block),
            pl.BlockSpec((1, SINKS, half), sink_block),
        ],
        req_local,
        heads_half,
        span_total,
    )

    def rows_of(x, owner):
        return lax.dynamic_slice_in_dim(x, owner * span_local, span_local, axis=2)

    def cache_rows(owner, normalize):
        first_row = jnp.reshape(owner * span_local, (1,)).astype(jnp.int32)
        q_block = lambda r, len_ref, win_ref, seq_ref, first_ref, owner_ref: (r, owner_ref[0], 0)
        span_block = lambda r, len_ref, win_ref, seq_ref, first_ref, owner_ref: (
            r,
            0,
            owner_ref[0],
            0,
        )
        grid_spec = pltpu.PrefetchScalarGridSpec(
            num_scalar_prefetch=5,
            grid=(req_local,),
            in_specs=[
                pl.BlockSpec((1, span_local, half), q_block),
                pl.BlockSpec((1, span_local, half), q_block),
                pl.BlockSpec((1, slot_local, local_cols), head_block),
                pl.BlockSpec((1, slot_local, local_cols), head_block),
                pl.BlockSpec((1, heads_half, span_local, HEAD_DIM), span_block),
                pl.BlockSpec((1, heads_half, span_local, 1), span_block),
                pl.BlockSpec((1, heads_half, span_local, 1), span_block),
            ],
            out_specs=[
                pl.BlockSpec((1, heads_local, span_local, HEAD_DIM), lambda r, *_: (r, 0, 0, 0)),
                pl.BlockSpec((1, heads_local, span_local, 2), lambda r, *_: (r, 0, 0, 0)),
            ],
        )
        shape = (req_local, heads_local, span_local)
        return pl.pallas_call(
            functools.partial(
                merged_cache_kernel, scaling=HEAD_DIM ** (-0.5), normalize=normalize
            ),
            grid_spec=grid_spec,
            out_shape=[
                jax.ShapeDtypeStruct(
                    shape + (HEAD_DIM,), jnp.bfloat16 if normalize else jnp.float32
                ),
                jax.ShapeDtypeStruct(shape + (2,), jnp.float32),
            ],
        )(
            cache_len,
            window_len,
            seq_arr,
            first_row,
            jnp.reshape(owner, (1,)).astype(jnp.int32),
            q_half,
            q_other,
            cache_keys,
            cache_values,
            *span_part,
        )

    far_norm, far_stats = cache_rows(1 - seq_index, True)
    got_norm = swap_seq(far_norm)
    got_stats = swap_seq(far_stats)
    own_sum, own_stats = cache_rows(seq_index, False)
    own_rows = (own_sum, own_stats[..., 0:1], own_stats[..., 1:2])
    got_total = got_stats[..., 1:2]
    got_sum = got_norm.astype(jnp.float32) * got_total
    total_sum, _, total = merge_parts(own_rows, (got_sum, got_stats[..., 0:1], got_total))
    own_offsets = seq_index * span_local + jnp.arange(span_local, dtype=jnp.int32)
    live_rows = (own_offsets[None, :] < span_len[:, None])[:, None, :, None]
    safe_total = jnp.where(live_rows, total, 1.0)
    mixed = jnp.where(live_rows, total_sum / safe_total, 0.0)
    return (
        mixed.transpose(0, 2, 1, 3).reshape(req_local, span_local, local_cols).astype(jnp.bfloat16)
    )


def solution(mesh):
    placed = (
        P("req", "seq", None),
        P(("req", "seq"), "tp"),
        P(("req", "seq"), "tp"),
        P(("req", "seq"), "tp"),
        P("tp"),
        P("tp"),
        P("req", "seq", "tp"),
        P("req", "seq", "tp"),
        P("req", None, "tp"),
        P("req", None, "tp"),
        P("req", None),
        P("req"),
        P("req"),
        P("req"),
    )
    body = on_device_pair if mesh.shape["seq"] == 2 else on_device
    return jax.shard_map(
        body, mesh=mesh, in_specs=placed, out_specs=P("req", "seq", "tp"), check_vma=False
    )
```

```python
import functools

import jax
import jax.numpy as jnp
from jax import lax
from jax.experimental import pallas as pl
from jax.experimental.pallas import tpu as pltpu
from jax.sharding import PartitionSpec as P

D = 2048
HEAD_DIM = 128
WINDOW = 4096
SINKS = 4


rope_base = 500000.0
epsilon = 1e-06
lowest = -1e30


def rotate_heads(vectors, positions):
    half_dim = vectors.shape[-1] // 2
    powers = jnp.arange(half_dim, dtype=jnp.float32) * (2.0 / vectors.shape[-1])
    inverse = rope_base ** (-powers)
    angles = positions.astype(jnp.float32)[:, None] * inverse[None, :]
    cosine = jnp.cos(angles)[:, None, :]
    sine_part = jnp.sin(angles)[:, None, :]
    leading = vectors[..., :half_dim]
    trailing = vectors[..., half_dim:]
    return jnp.concatenate(
        [leading * cosine - trailing * sine_part, trailing * cosine + leading * sine_part], axis=-1
    )


def normalize_rotate(projected, squares, feature_gain, positions, model_width, head_size):
    factor = lax.rsqrt(squares / model_width + epsilon)
    normed = projected * factor[:, None] * feature_gain[None, :]
    shaped = normed.reshape(projected.shape[0], projected.shape[1] // head_size, head_size)
    return rotate_heads(shaped, positions).reshape(projected.shape).astype(jnp.bfloat16)


def cache_kernel(len_ref, win_ref, seq_ref, q_ref, ck_ref, cv_ref, o_ref, m_ref, l_ref, *, scaling):
    r = pl.program_id(0)
    length_now = len_ref[r]
    window_now = win_ref[r]
    seq_index = seq_ref[0]
    seq_count, _, span_local, _ = q_ref.shape
    slots = ck_ref.shape[1]
    keys = ck_ref[0]
    values = cv_ref[0]
    dims = (((1,), (1,)), ((), ()))
    row = lax.broadcasted_iota(jnp.int32, (span_local, slots), 0)
    slot = lax.broadcasted_iota(jnp.int32, (span_local, slots), 1) + seq_index * slots
    slot_pos = length_now - 1 - ((length_now - 1 - slot) & (WINDOW - 1))
    for shift in range(seq_count):
        owner = (seq_index - shift + seq_count) % seq_count
        scores = (
            lax.dot_general(q_ref[shift, 0], keys, dims, preferred_element_type=jnp.float32)
            * scaling
        )
        edge = length_now + owner * span_local + row - window_now
        allowed = (slot_pos >= 0) & (slot_pos > edge)
        highest = jnp.max(jnp.where(allowed, scores, lowest), axis=1, keepdims=True)
        weights = jnp.where(allowed, jnp.exp(scores - highest), 0.0)
        o_ref[shift, 0, 0] = jnp.dot(
            weights.astype(jnp.bfloat16), values, preferred_element_type=jnp.float32
        )
        m_ref[shift, 0, 0] = highest
        l_ref[shift, 0, 0] = jnp.sum(weights, axis=1, keepdims=True)


def cache_attention(q_parts, cache_keys, cache_values, cache_len, window_len, seq_index):
    seq_count, req_local, span_local, local_cols = q_parts.shape
    heads_local = local_cols // HEAD_DIM
    slot_local = cache_keys.shape[1]
    kernel = functools.partial(cache_kernel, scaling=HEAD_DIM ** (-0.5))
    part = (seq_count, 1, 1, span_local)
    grid_spec = pltpu.PrefetchScalarGridSpec(
        num_scalar_prefetch=3,
        grid=(req_local, heads_local),
        in_specs=[
            pl.BlockSpec((seq_count, 1, span_local, HEAD_DIM), lambda r, h, *_: (0, r, 0, h)),
            pl.BlockSpec((1, slot_local, HEAD_DIM), lambda r, h, *_: (r, 0, h)),
            pl.BlockSpec((1, slot_local, HEAD_DIM), lambda r, h, *_: (r, 0, h)),
        ],
        out_specs=[
            pl.BlockSpec(part + (HEAD_DIM,), lambda r, h, *_: (0, r, h, 0, 0)),
            pl.BlockSpec(part + (1,), lambda r, h, *_: (0, r, h, 0, 0)),
            pl.BlockSpec(part + (1,), lambda r, h, *_: (0, r, h, 0, 0)),
        ],
    )
    shape = (seq_count, req_local, heads_local, span_local)
    return pl.pallas_call(
        kernel,
        grid_spec=grid_spec,
        out_shape=[
            jax.ShapeDtypeStruct(shape + (HEAD_DIM,), jnp.float32),
            jax.ShapeDtypeStruct(shape + (1,), jnp.float32),
            jax.ShapeDtypeStruct(shape + (1,), jnp.float32),
        ],
    )(
        cache_len,
        window_len,
        jnp.reshape(seq_index, (1,)).astype(jnp.int32),
        q_parts,
        cache_keys,
        cache_values,
    )


def span_kernel(
    len_ref,
    win_ref,
    seq_ref,
    live_ref,
    sink_pos_ref,
    q_ref,
    nk_ref,
    nv_ref,
    sk_ref,
    sv_ref,
    ps_ref,
    pst_ref,
    out_ref,
    *,
    scaling,
):
    r = pl.program_id(0)
    length_now = len_ref[r]
    window_now = win_ref[r]
    seq_index = seq_ref[0]
    live_count = live_ref[r]
    seq_count, _, span_local, _ = nk_ref.shape
    queries = q_ref[0]
    dims = (((1,), (1,)), ((), ()))
    row = lax.broadcasted_iota(jnp.int32, (span_local, span_local), 0) + seq_index * span_local
    col = lax.broadcasted_iota(jnp.int32, (span_local, span_local), 1)
    span_scores, span_ok = [], []
    for shift in range(seq_count):
        owner = (seq_index - shift + seq_count) % seq_count
        span_scores.append(
            lax.dot_general(queries, nk_ref[shift, 0], dims, preferred_element_type=jnp.float32)
            * scaling
        )
        span_ok.append(owner * span_local + col <= row)
    query_f = queries.astype(jnp.float32)
    row_1 = lax.broadcasted_iota(jnp.int32, (span_local, 1), 0) + seq_index * span_local
    edge = length_now + row_1 - window_now
    sink_scores, sink_ok = [], []
    for sink in range(SINKS):
        key_f = sk_ref[0, sink : sink + 1, :].astype(jnp.float32)
        sink_scores.append(jnp.sum(query_f * key_f, axis=1, keepdims=True) * scaling)
        sink_ok.append(sink_pos_ref[r * SINKS + sink] <= edge)
    part_high = pst_ref[:, 0, 0, :, 0:1]
    part_total = pst_ref[:, 0, 0, :, 1:2]
    peak = jnp.max(part_high, axis=0)
    for scores, ok in zip(span_scores + sink_scores, span_ok + sink_ok):
        peak = jnp.maximum(peak, jnp.max(jnp.where(ok, scores, lowest), axis=1, keepdims=True))
    factor = jnp.exp(part_high - peak[None])
    denominator = jnp.sum(part_total * factor, axis=0)
    numerator = jnp.sum(ps_ref[:, 0, 0] * factor, axis=0)
    for shift in range(seq_count):
        weights = jnp.where(span_ok[shift], jnp.exp(span_scores[shift] - peak), 0.0)
        denominator = denominator + jnp.sum(weights, axis=1, keepdims=True)
        numerator = numerator + jnp.dot(
            weights.astype(jnp.bfloat16), nv_ref[shift, 0], preferred_element_type=jnp.float32
        )
    for sink in range(SINKS):
        weights = jnp.where(sink_ok[sink], jnp.exp(sink_scores[sink] - peak), 0.0)
        denominator = denominator + weights
        value_f = sv_ref[0, sink : sink + 1, :].astype(jnp.float32)
        numerator = numerator + weights.astype(jnp.bfloat16).astype(jnp.float32) * value_f
    live = row_1 < live_count
    safe = jnp.where(live, denominator, 1.0)
    out_ref[0] = jnp.where(live, numerator / safe, 0.0).astype(out_ref.dtype)


def span_attention(
    q_local, kv_parts, sink_keys, sink_values, parts_sum, parts_stats, scalars
):
    req_local, span_local, local_cols = q_local.shape
    seq_count = kv_parts.shape[0]
    heads_local = local_cols // HEAD_DIM
    kernel = functools.partial(span_kernel, scaling=HEAD_DIM ** (-0.5))
    part = (seq_count, 1, 1, span_local)
    grid_spec = pltpu.PrefetchScalarGridSpec(
        num_scalar_prefetch=5,
        grid=(req_local, heads_local),
        in_specs=[
            pl.BlockSpec((1, span_local, HEAD_DIM), lambda r, h, *_: (r, 0, h)),
            pl.BlockSpec((seq_count, 1, span_local, HEAD_DIM), lambda r, h, *_: (0, r, 0, h)),
            pl.BlockSpec(
                (seq_count, 1, span_local, HEAD_DIM),
                lambda r, h, *_: (0, r, 0, h + heads_local),
            ),
            pl.BlockSpec((1, SINKS, HEAD_DIM), lambda r, h, *_: (r, 0, h)),
            pl.BlockSpec((1, SINKS, HEAD_DIM), lambda r, h, *_: (r, 0, h)),
            pl.BlockSpec(part + (HEAD_DIM,), lambda r, h, *_: (0, r, h, 0, 0)),
            pl.BlockSpec(part + (2,), lambda r, h, *_: (0, r, h, 0, 0)),
        ],
        out_specs=pl.BlockSpec((1, span_local, HEAD_DIM), lambda r, h, *_: (r, 0, h)),
    )
    return pl.pallas_call(
        kernel,
        grid_spec=grid_spec,
        out_shape=jax.ShapeDtypeStruct((req_local, span_local, local_cols), jnp.bfloat16),
    )(*scalars, q_local, kv_parts, kv_parts, sink_keys, sink_values, parts_sum, parts_stats)


def shifted(x, axis_name, shift):
    count = lax.axis_size(axis_name)
    if shift % count == 0:
        return x
    return lax.ppermute(x, axis_name, [(a, (a + shift) % count) for a in range(count)])


def tp_sum(x):
    count = lax.axis_size("tp")
    assert count & (count - 1) == 0
    bit = 1
    while bit < count:
        x = x + lax.ppermute(x, "tp", [(a, a ^ bit) for a in range(count)])
        bit *= 2
    return x


def on_device(
    tokens,
    w_query,
    w_key,
    w_value,
    q_gain,
    k_gain,
    cache_keys,
    cache_values,
    sink_keys,
    sink_values,
    sink_pos,
    cache_len,
    span_len,
    window_len,
):
    req_local, span_local, model_width = tokens.shape
    local_cols = w_query.shape[1]
    seq_count = lax.axis_size("seq")
    seq_index = lax.axis_index("seq")
    token_rows = tokens.reshape(req_local * span_local, model_width)
    offsets = seq_index * span_local + jnp.arange(span_local, dtype=jnp.int32)
    positions = (cache_len[:, None] + offsets[None, :]).reshape(-1)
    wq_all = lax.all_gather(w_query, ("req", "seq"), axis=0, tiled=True)
    wkv_all = lax.all_gather(
        jnp.concatenate([w_key, w_value], axis=1), ("req", "seq"), axis=0, tiled=True
    )
    q_proj = jnp.dot(token_rows, wq_all, preferred_element_type=jnp.float32)
    q_squares = tp_sum(jnp.sum(q_proj * q_proj, axis=1))
    q_local = normalize_rotate(q_proj, q_squares, q_gain, positions, D, HEAD_DIM).reshape(
        req_local, span_local, local_cols
    )
    q_parts = jnp.stack([shifted(q_local, "seq", shift) for shift in range(seq_count)])
    c_sum, c_high, c_total = cache_attention(
        q_parts, cache_keys, cache_values, cache_len, window_len, seq_index
    )
    c_stats = jnp.concatenate([c_high, c_total], axis=-1)
    parts_sum = jnp.stack([shifted(c_sum[s], "seq", -s) for s in range(seq_count)])
    parts_stats = jnp.stack([shifted(c_stats[s], "seq", -s) for s in range(seq_count)])
    wkv_all, parts_sum, parts_stats = lax.optimization_barrier((wkv_all, parts_sum, parts_stats))
    kv_proj = jnp.dot(token_rows, wkv_all, preferred_element_type=jnp.float32)
    k_proj = kv_proj[:, :local_cols]
    k_squares = tp_sum(jnp.sum(k_proj * k_proj, axis=1))
    k_rot = normalize_rotate(k_proj, k_squares, k_gain, positions, D, HEAD_DIM)
    v_new = kv_proj[:, local_cols:].astype(jnp.bfloat16)
    kv_new = jnp.concatenate([k_rot, v_new], axis=1).reshape(req_local, span_local, 2 * local_cols)
    kv_parts = jnp.stack([shifted(kv_new, "seq", shift) for shift in range(seq_count)])
    scalars = (
        cache_len,
        window_len,
        jnp.reshape(seq_index, (1,)).astype(jnp.int32),
        span_len,
        sink_pos.reshape(-1),
    )
    return span_attention(
        q_local, kv_parts, sink_keys, sink_values, parts_sum, parts_stats, scalars
    )


def pair_cache_kernel(
    len_ref, win_ref, seq_ref, first_ref, q_ref, ck_ref, cv_ref, o_ref, m_ref, l_ref, *, scaling
):
    r = pl.program_id(0)
    length_now = len_ref[r] + first_ref[0]
    window_now = win_ref[r]
    seq_index = seq_ref[0]
    rows, slots = q_ref.shape[1], ck_ref.shape[1]
    heads = q_ref.shape[2] // HEAD_DIM
    dims = (((1,), (1,)), ((), ()))
    row = lax.broadcasted_iota(jnp.int32, (rows, slots), 0)
    slot = lax.broadcasted_iota(jnp.int32, (rows, slots), 1) + seq_index * slots
    edge = length_now + row - window_now
    slot_pos = length_now - 1 - ((length_now - 1 - slot) & (WINDOW - 1))
    allowed = (slot_pos >= 0) & (slot_pos > edge)
    bias = jnp.where(allowed, 0.0, lowest)
    for h in range(heads):
        cols = slice(h * HEAD_DIM, (h + 1) * HEAD_DIM)
        scores = (
            lax.dot_general(q_ref[0, :, cols], ck_ref[0, :, cols], dims, preferred_element_type=jnp.float32)
            * scaling
            + bias
        )
        highest = jnp.max(scores, axis=1, keepdims=True)
        weights = jnp.exp(scores - highest)
        some = highest > lowest
        o_ref[0, h] = jnp.where(
            some,
            jnp.dot(weights.astype(jnp.bfloat16), cv_ref[0, :, cols], preferred_element_type=jnp.float32),
            0.0,
        )
        m_ref[0, h] = highest
        l_ref[0, h] = jnp.where(some, jnp.sum(weights, axis=1, keepdims=True), 0.0)


def pair_span_kernel(
    len_ref, win_ref, sink_pos_ref, seq_ref, q_ref, nk_ref, nv_ref, sk_ref, sv_ref, o_ref, m_ref, l_ref, *, scaling
):
    r = pl.program_id(0)
    length_now = len_ref[r]
    window_now = win_ref[r]
    rows = q_ref.shape[1]
    heads = q_ref.shape[2] // HEAD_DIM
    dims = (((1,), (1,)), ((), ()))
    row = lax.broadcasted_iota(jnp.int32, (rows, rows), 0)
    key = lax.broadcasted_iota(jnp.int32, (rows, rows), 1)
    allowed = key <= row
    row_1 = lax.broadcasted_iota(jnp.int32, (rows, 1), 0)
    edge = length_now + row_1 - window_now
    sink_ok = [sink_pos_ref[r * SINKS + sink] <= edge for sink in range(SINKS)]
    for h in range(heads):
        cols = slice(h * HEAD_DIM, (h + 1) * HEAD_DIM)
        queries = q_ref[0, :, cols]
        scores = (
            lax.dot_general(queries, nk_ref[0, :, cols], dims, preferred_element_type=jnp.float32)
            * scaling
        )
        query_f = queries.astype(jnp.float32)
        sink_scores = []
        for sink in range(SINKS):
            key_f = sk_ref[0, sink : sink + 1, cols].astype(jnp.float32)
            sink_scores.append(jnp.sum(query_f * key_f, axis=1, keepdims=True) * scaling)
        highest = jnp.max(jnp.where(allowed, scores, lowest), axis=1, keepdims=True)
        for part, ok in zip(sink_scores, sink_ok):
            highest = jnp.maximum(highest, jnp.where(ok, part, lowest))
        weights = jnp.where(allowed, jnp.exp(scores - highest), 0.0)
        totals = jnp.sum(weights, axis=1, keepdims=True)
        summed = jnp.dot(
            weights.astype(jnp.bfloat16), nv_ref[0, :, cols], preferred_element_type=jnp.float32
        )
        for sink in range(SINKS):
            sink_w = jnp.where(sink_ok[sink], jnp.exp(sink_scores[sink] - highest), 0.0)
            totals = totals + sink_w
            value_f = sv_ref[0, sink : sink + 1, cols].astype(jnp.float32)
            summed = summed + sink_w.astype(jnp.bfloat16).astype(jnp.float32) * value_f
        o_ref[0, h] = summed
        m_ref[0, h] = highest
        l_ref[0, h] = totals


def merged_cache_kernel(
    len_ref, win_ref, seq_ref, first_ref, owner_ref, qa_ref, qb_ref, ck_ref, cv_ref, ss_ref, sm_ref,
    sl_ref, o_ref, st_ref, *, scaling, normalize
):
    r = pl.program_id(0)
    length_now = len_ref[r] + first_ref[0]
    window_now = win_ref[r]
    seq_index = seq_ref[0]
    rows, slots = qa_ref.shape[1], ck_ref.shape[1]
    heads_half = ss_ref.shape[1]
    heads = 2 * heads_half
    dims = (((1,), (1,)), ((), ()))
    row = lax.broadcasted_iota(jnp.int32, (rows, slots), 0)
    slot = lax.broadcasted_iota(jnp.int32, (rows, slots), 1) + seq_index * slots
    edge = length_now + row - window_now
    cached = len_ref[r]
    slot_pos = cached - 1 - ((cached - 1 - slot) & (WINDOW - 1))
    allowed = (slot_pos >= 0) & (slot_pos > edge)
    bias = jnp.where(allowed, 0.0, lowest)
    for h in range(heads):
        cols = slice(h * HEAD_DIM, (h + 1) * HEAD_DIM)
        j = h % heads_half
        local = slice(j * HEAD_DIM, (j + 1) * HEAD_DIM)
        here = (h // heads_half) == seq_index
        queries = jnp.where(here, qa_ref[0, :, local], qb_ref[0, :, local])
        scores = (
            lax.dot_general(queries, ck_ref[0, :, cols], dims, preferred_element_type=jnp.float32)
            * scaling
            + bias
        )
        highest = jnp.max(scores, axis=1, keepdims=True)
        weights = jnp.exp(scores - highest)
        some = highest > lowest
        summed = jnp.where(
            some,
            jnp.dot(weights.astype(jnp.bfloat16), cv_ref[0, :, cols], preferred_element_type=jnp.float32),
            0.0,
        )
        totals = jnp.where(some, jnp.sum(weights, axis=1, keepdims=True), 0.0)
        span_high = sm_ref[0, j]
        peak = jnp.maximum(highest, span_high)
        f_cache = jnp.exp(highest - peak)
        f_span = jnp.exp(span_high - peak)
        summed = jnp.where(here, summed * f_cache + ss_ref[0, j] * f_span, summed)
        totals = jnp.where(here, totals * f_cache + sl_ref[0, j] * f_span, totals)
        highest = jnp.where(here, peak, highest)
        if normalize:
            summed = summed / jnp.where(totals > 0, totals, 1.0)
        o_ref[0, :, cols] = summed.astype(o_ref.dtype)
        st_ref[0, h, :, 0:1] = highest
        st_ref[0, h, :, 1:2] = totals


def pair_partials(kernel, scalars, q_spec_index, operands, in_specs, req_local, heads, rows):
    grid_spec = pltpu.PrefetchScalarGridSpec(
        num_scalar_prefetch=len(scalars),
        grid=(req_local,),
        in_specs=in_specs,
        out_specs=[
            pl.BlockSpec((1, heads, rows, HEAD_DIM), lambda r, *_: (r, 0, 0, 0)),
            pl.BlockSpec((1, heads, rows, 1), lambda r, *_: (r, 0, 0, 0)),
            pl.BlockSpec((1, heads, rows, 1), lambda r, *_: (r, 0, 0, 0)),
        ],
    )
    shape = (req_local, heads, rows)
    return pl.pallas_call(
        functools.partial(kernel, scaling=HEAD_DIM ** (-0.5)),
        grid_spec=grid_spec,
        out_shape=[
            jax.ShapeDtypeStruct(shape + (HEAD_DIM,), jnp.float32),
            jax.ShapeDtypeStruct(shape + (1,), jnp.float32),
            jax.ShapeDtypeStruct(shape + (1,), jnp.float32),
        ],
    )(*scalars, *operands)


def merge_parts(first, second):
    s1, m1, l1 = first
    s2, m2, l2 = second
    peak = jnp.maximum(m1, m2)
    f1 = jnp.exp(m1 - peak)
    f2 = jnp.exp(m2 - peak)
    return (s1 * f1 + s2 * f2, peak, l1 * f1 + l2 * f2)


def swap_seq(x):
    return lax.ppermute(x, "seq", [(0, 1), (1, 0)])


def on_device_pair(
    tokens,
    w_query,
    w_key,
    w_value,
    q_gain,
    k_gain,
    cache_keys,
    cache_values,
    sink_keys,
    sink_values,
    sink_pos,
    cache_len,
    span_len,
    window_len,
):
    req_local, span_local, model_width = tokens.shape
    local_cols = w_query.shape[1]
    half = local_cols // 2
    heads_local = local_cols // HEAD_DIM
    heads_half = heads_local // 2
    seq_index = lax.axis_index("seq")
    first = seq_index == 0
    span_total = 2 * span_local
    slot_local = cache_keys.shape[1]
    weights = (w_query, w_key, w_value)
    other = jnp.concatenate(
        [jnp.where(first, w[:, half:], w[:, :half]) for w in weights], axis=1
    )
    got = swap_seq(other)
    mine = jnp.concatenate(
        [jnp.where(first, w[:, :half], w[:, half:]) for w in weights], axis=1
    )
    w_all = lax.all_gather(jnp.concatenate([mine, got], 0), "req", axis=0, tiled=True)
    tokens_other = swap_seq(tokens)
    tokens_all = jnp.where(
        first,
        jnp.concatenate([tokens, tokens_other], axis=1),
        jnp.concatenate([tokens_other, tokens], axis=1),
    )
    row_block = w_query.shape[0]
    blocks = tokens_all.reshape(req_local, span_total, model_width // (2 * row_block), 2, row_block)
    tokens_all = jnp.where(first, blocks, blocks[:, :, :, ::-1, :]).reshape(tokens_all.shape)
    token_rows = tokens_all.reshape(req_local * span_total, model_width)
    proj = jnp.dot(token_rows, w_all, preferred_element_type=jnp.float32)
    q_proj = proj[:, :half]
    k_proj = proj[:, half : 2 * half]
    v_proj = proj[:, 2 * half :]
    squares = jnp.stack([jnp.sum(q_proj * q_proj, axis=1), jnp.sum(k_proj * k_proj, axis=1)])
    squares = tp_sum(squares)
    squares = squares + swap_seq(squares)
    offsets = jnp.arange(span_total, dtype=jnp.int32)
    positions = (cache_len[:, None] + offsets[None, :]).reshape(-1)
    q_gain_half = lax.dynamic_slice_in_dim(q_gain, seq_index * half, half)
    k_gain_half = lax.dynamic_slice_in_dim(k_gain, seq_index * half, half)
    q_half = normalize_rotate(q_proj, squares[0], q_gain_half, positions, D, HEAD_DIM).reshape(
        req_local, span_total, half
    )
    k_half = normalize_rotate(k_proj, squares[1], k_gain_half, positions, D, HEAD_DIM).reshape(
        req_local, span_total, half
    )
    v_half = v_proj.astype(jnp.bfloat16).reshape(req_local, span_total, half)
    q_other = swap_seq(q_half)
    q_full = jnp.where(
        first, jnp.concatenate([q_half, q_other], -1), jnp.concatenate([q_other, q_half], -1)
    )
    seq_arr = jnp.reshape(seq_index, (1,)).astype(jnp.int32)
    head_block = lambda r, *_: (r, 0, 0)
    sink_block = lambda r, len_ref, win_ref, pos_ref, seq_ref: (r, 0, seq_ref[0])
    span_part = pair_partials(
        pair_span_kernel,
        (cache_len, window_len, sink_pos.reshape(-1), seq_arr),
        None,
        (q_half, k_half, v_half, sink_keys, sink_values),
        [
            pl.BlockSpec((1, span_total, half), head_block),
            pl.BlockSpec((1, span_total, half), head_block),
            pl.BlockSpec((1, span_total, half), head_block),
            pl.BlockSpec((1, SINKS, half), sink_block),
            pl.BlockSpec((1, SINKS, half), sink_block),
        ],
        req_local,
        heads_half,
        span_total,
    )

    def rows_of(x, owner):
        return lax.dynamic_slice_in_dim(x, owner * span_local, span_local, axis=2)

    def cache_rows(owner, normalize):
        first_row = jnp.reshape(owner * span_local, (1,)).astype(jnp.int32)
        q_block = lambda r, len_ref, win_ref, seq_ref, first_ref, owner_ref: (r, owner_ref[0], 0)
        span_block = lambda r, len_ref, win_ref, seq_ref, first_ref, owner_ref: (
            r,
            0,
            owner_ref[0],
            0,
        )
        grid_spec = pltpu.PrefetchScalarGridSpec(
            num_scalar_prefetch=5,
            grid=(req_local,),
            in_specs=[
                pl.BlockSpec((1, span_local, half), q_block),
                pl.BlockSpec((1, span_local, half), q_block),
                pl.BlockSpec((1, slot_local, local_cols), head_block),
                pl.BlockSpec((1, slot_local, local_cols), head_block),
                pl.BlockSpec((1, heads_half, span_local, HEAD_DIM), span_block),
                pl.BlockSpec((1, heads_half, span_local, 1), span_block),
                pl.BlockSpec((1, heads_half, span_local, 1), span_block),
            ],
            out_specs=[
                pl.BlockSpec((1, span_local, local_cols), lambda r, *_: (r, 0, 0)),
                pl.BlockSpec((1, heads_local, span_local, 2), lambda r, *_: (r, 0, 0, 0)),
            ],
        )
        shape = (req_local, heads_local, span_local)
        return pl.pallas_call(
            functools.partial(
                merged_cache_kernel, scaling=HEAD_DIM ** (-0.5), normalize=normalize
            ),
            grid_spec=grid_spec,
            out_shape=[
                jax.ShapeDtypeStruct(
                    (req_local, span_local, local_cols),
                    jnp.bfloat16 if normalize else jnp.float32,
                ),
                jax.ShapeDtypeStruct(shape + (2,), jnp.float32),
            ],
        )(
            cache_len,
            window_len,
            seq_arr,
            first_row,
            jnp.reshape(owner, (1,)).astype(jnp.int32),
            q_half,
            q_other,
            cache_keys,
            cache_values,
            *span_part,
        )

    far_norm, far_stats = cache_rows(1 - seq_index, True)
    got_norm = swap_seq(far_norm)
    got_stats = swap_seq(far_stats)
    own_sum, own_stats = cache_rows(seq_index, False)
    own_high, own_total = own_stats[..., 0], own_stats[..., 1]
    got_high, got_total = got_stats[..., 0], got_stats[..., 1]
    peak = jnp.maximum(own_high, got_high)
    own_factor = jnp.exp(own_high - peak)
    got_factor = jnp.exp(got_high - peak) * got_total
    total = own_total * own_factor + got_factor

    def per_row(x):
        return jnp.transpose(x, (0, 2, 1))[..., None]

    heads_shape = (req_local, span_local, heads_local, HEAD_DIM)
    total_sum = own_sum.reshape(heads_shape) * per_row(own_factor) + got_norm.reshape(
        heads_shape
    ).astype(jnp.float32) * per_row(got_factor)
    own_offsets = seq_index * span_local + jnp.arange(span_local, dtype=jnp.int32)
    live_rows = (own_offsets[None, :] < span_len[:, None])[:, :, None, None]
    safe_total = jnp.where(live_rows, per_row(total), 1.0)
    mixed = jnp.where(live_rows, total_sum / safe_total, 0.0)
    return mixed.reshape(req_local, span_local, local_cols).astype(jnp.bfloat16)


def solution(mesh):
    placed = (
        P("req", "seq", None),
        P(("req", "seq"), "tp"),
        P(("req", "seq"), "tp"),
        P(("req", "seq"), "tp"),
        P("tp"),
        P("tp"),
        P("req", "seq", "tp"),
        P("req", "seq", "tp"),
        P("req", None, "tp"),
        P("req", None, "tp"),
        P("req", None),
        P("req"),
        P("req"),
        P("req"),
    )
    body = on_device_pair if mesh.shape["seq"] == 2 else on_device
    return jax.shard_map(
        body, mesh=mesh, in_specs=placed, out_specs=P("req", "seq", "tp"), check_vma=False
    )
```

```python
import functools

import jax
import jax.numpy as jnp
from jax import lax
from jax.experimental import pallas as pl
from jax.experimental.pallas import tpu as pltpu
from jax.sharding import PartitionSpec as P

D = 2048
HEAD_DIM = 128
WINDOW = 4096
SINKS = 4


rope_base = 500000.0
epsilon = 1e-06
lowest = -1e30


def rotate_heads(vectors, positions):
    half_dim = vectors.shape[-1] // 2
    powers = jnp.arange(half_dim, dtype=jnp.float32) * (2.0 / vectors.shape[-1])
    inverse = rope_base ** (-powers)
    angles = positions.astype(jnp.float32)[:, None] * inverse[None, :]
    cosine = jnp.cos(angles)[:, None, :]
    sine_part = jnp.sin(angles)[:, None, :]
    leading = vectors[..., :half_dim]
    trailing = vectors[..., half_dim:]
    return jnp.concatenate(
        [leading * cosine - trailing * sine_part, trailing * cosine + leading * sine_part], axis=-1
    )


def normalize_rotate(projected, squares, feature_gain, positions, model_width, head_size):
    factor = lax.rsqrt(squares / model_width + epsilon)
    normed = projected * factor[:, None] * feature_gain[None, :]
    shaped = normed.reshape(projected.shape[0], projected.shape[1] // head_size, head_size)
    return rotate_heads(shaped, positions).reshape(projected.shape).astype(jnp.bfloat16)


def cache_kernel(len_ref, win_ref, seq_ref, q_ref, ck_ref, cv_ref, o_ref, m_ref, l_ref, *, scaling):
    r = pl.program_id(0)
    length_now = len_ref[r]
    window_now = win_ref[r]
    seq_index = seq_ref[0]
    seq_count, _, span_local, _ = q_ref.shape
    slots = ck_ref.shape[1]
    keys = ck_ref[0]
    values = cv_ref[0]
    dims = (((1,), (1,)), ((), ()))
    row = lax.broadcasted_iota(jnp.int32, (span_local, slots), 0)
    slot = lax.broadcasted_iota(jnp.int32, (span_local, slots), 1) + seq_index * slots
    slot_pos = length_now - 1 - ((length_now - 1 - slot) & (WINDOW - 1))
    for shift in range(seq_count):
        owner = (seq_index - shift + seq_count) % seq_count
        scores = (
            lax.dot_general(q_ref[shift, 0], keys, dims, preferred_element_type=jnp.float32)
            * scaling
        )
        edge = length_now + owner * span_local + row - window_now
        allowed = (slot_pos >= 0) & (slot_pos > edge)
        highest = jnp.max(jnp.where(allowed, scores, lowest), axis=1, keepdims=True)
        weights = jnp.where(allowed, jnp.exp(scores - highest), 0.0)
        o_ref[shift, 0, 0] = jnp.dot(
            weights.astype(jnp.bfloat16), values, preferred_element_type=jnp.float32
        )
        m_ref[shift, 0, 0] = highest
        l_ref[shift, 0, 0] = jnp.sum(weights, axis=1, keepdims=True)


def cache_attention(q_parts, cache_keys, cache_values, cache_len, window_len, seq_index):
    seq_count, req_local, span_local, local_cols = q_parts.shape
    heads_local = local_cols // HEAD_DIM
    slot_local = cache_keys.shape[1]
    kernel = functools.partial(cache_kernel, scaling=HEAD_DIM ** (-0.5))
    part = (seq_count, 1, 1, span_local)
    grid_spec = pltpu.PrefetchScalarGridSpec(
        num_scalar_prefetch=3,
        grid=(req_local, heads_local),
        in_specs=[
            pl.BlockSpec((seq_count, 1, span_local, HEAD_DIM), lambda r, h, *_: (0, r, 0, h)),
            pl.BlockSpec((1, slot_local, HEAD_DIM), lambda r, h, *_: (r, 0, h)),
            pl.BlockSpec((1, slot_local, HEAD_DIM), lambda r, h, *_: (r, 0, h)),
        ],
        out_specs=[
            pl.BlockSpec(part + (HEAD_DIM,), lambda r, h, *_: (0, r, h, 0, 0)),
            pl.BlockSpec(part + (1,), lambda r, h, *_: (0, r, h, 0, 0)),
            pl.BlockSpec(part + (1,), lambda r, h, *_: (0, r, h, 0, 0)),
        ],
    )
    shape = (seq_count, req_local, heads_local, span_local)
    return pl.pallas_call(
        kernel,
        grid_spec=grid_spec,
        out_shape=[
            jax.ShapeDtypeStruct(shape + (HEAD_DIM,), jnp.float32),
            jax.ShapeDtypeStruct(shape + (1,), jnp.float32),
            jax.ShapeDtypeStruct(shape + (1,), jnp.float32),
        ],
    )(
        cache_len,
        window_len,
        jnp.reshape(seq_index, (1,)).astype(jnp.int32),
        q_parts,
        cache_keys,
        cache_values,
    )


def span_kernel(
    len_ref,
    win_ref,
    seq_ref,
    live_ref,
    sink_pos_ref,
    q_ref,
    nk_ref,
    nv_ref,
    sk_ref,
    sv_ref,
    ps_ref,
    pst_ref,
    out_ref,
    *,
    scaling,
):
    r = pl.program_id(0)
    length_now = len_ref[r]
    window_now = win_ref[r]
    seq_index = seq_ref[0]
    live_count = live_ref[r]
    seq_count, _, span_local, _ = nk_ref.shape
    queries = q_ref[0]
    dims = (((1,), (1,)), ((), ()))
    row = lax.broadcasted_iota(jnp.int32, (span_local, span_local), 0) + seq_index * span_local
    col = lax.broadcasted_iota(jnp.int32, (span_local, span_local), 1)
    span_scores, span_ok = [], []
    for shift in range(seq_count):
        owner = (seq_index - shift + seq_count) % seq_count
        span_scores.append(
            lax.dot_general(queries, nk_ref[shift, 0], dims, preferred_element_type=jnp.float32)
            * scaling
        )
        span_ok.append(owner * span_local + col <= row)
    query_f = queries.astype(jnp.float32)
    row_1 = lax.broadcasted_iota(jnp.int32, (span_local, 1), 0) + seq_index * span_local
    edge = length_now + row_1 - window_now
    sink_scores, sink_ok = [], []
    for sink in range(SINKS):
        key_f = sk_ref[0, sink : sink + 1, :].astype(jnp.float32)
        sink_scores.append(jnp.sum(query_f * key_f, axis=1, keepdims=True) * scaling)
        sink_ok.append(sink_pos_ref[r * SINKS + sink] <= edge)
    part_high = pst_ref[:, 0, 0, :, 0:1]
    part_total = pst_ref[:, 0, 0, :, 1:2]
    peak = jnp.max(part_high, axis=0)
    for scores, ok in zip(span_scores + sink_scores, span_ok + sink_ok):
        peak = jnp.maximum(peak, jnp.max(jnp.where(ok, scores, lowest), axis=1, keepdims=True))
    factor = jnp.exp(part_high - peak[None])
    denominator = jnp.sum(part_total * factor, axis=0)
    numerator = jnp.sum(ps_ref[:, 0, 0] * factor, axis=0)
    for shift in range(seq_count):
        weights = jnp.where(span_ok[shift], jnp.exp(span_scores[shift] - peak), 0.0)
        denominator = denominator + jnp.sum(weights, axis=1, keepdims=True)
        numerator = numerator + jnp.dot(
            weights.astype(jnp.bfloat16), nv_ref[shift, 0], preferred_element_type=jnp.float32
        )
    for sink in range(SINKS):
        weights = jnp.where(sink_ok[sink], jnp.exp(sink_scores[sink] - peak), 0.0)
        denominator = denominator + weights
        value_f = sv_ref[0, sink : sink + 1, :].astype(jnp.float32)
        numerator = numerator + weights.astype(jnp.bfloat16).astype(jnp.float32) * value_f
    live = row_1 < live_count
    safe = jnp.where(live, denominator, 1.0)
    out_ref[0] = jnp.where(live, numerator / safe, 0.0).astype(out_ref.dtype)


def span_attention(
    q_local, kv_parts, sink_keys, sink_values, parts_sum, parts_stats, scalars
):
    req_local, span_local, local_cols = q_local.shape
    seq_count = kv_parts.shape[0]
    heads_local = local_cols // HEAD_DIM
    kernel = functools.partial(span_kernel, scaling=HEAD_DIM ** (-0.5))
    part = (seq_count, 1, 1, span_local)
    grid_spec = pltpu.PrefetchScalarGridSpec(
        num_scalar_prefetch=5,
        grid=(req_local, heads_local),
        in_specs=[
            pl.BlockSpec((1, span_local, HEAD_DIM), lambda r, h, *_: (r, 0, h)),
            pl.BlockSpec((seq_count, 1, span_local, HEAD_DIM), lambda r, h, *_: (0, r, 0, h)),
            pl.BlockSpec(
                (seq_count, 1, span_local, HEAD_DIM),
                lambda r, h, *_: (0, r, 0, h + heads_local),
            ),
            pl.BlockSpec((1, SINKS, HEAD_DIM), lambda r, h, *_: (r, 0, h)),
            pl.BlockSpec((1, SINKS, HEAD_DIM), lambda r, h, *_: (r, 0, h)),
            pl.BlockSpec(part + (HEAD_DIM,), lambda r, h, *_: (0, r, h, 0, 0)),
            pl.BlockSpec(part + (2,), lambda r, h, *_: (0, r, h, 0, 0)),
        ],
        out_specs=pl.BlockSpec((1, span_local, HEAD_DIM), lambda r, h, *_: (r, 0, h)),
    )
    return pl.pallas_call(
        kernel,
        grid_spec=grid_spec,
        out_shape=jax.ShapeDtypeStruct((req_local, span_local, local_cols), jnp.bfloat16),
    )(*scalars, q_local, kv_parts, kv_parts, sink_keys, sink_values, parts_sum, parts_stats)


def shifted(x, axis_name, shift):
    count = lax.axis_size(axis_name)
    if shift % count == 0:
        return x
    return lax.ppermute(x, axis_name, [(a, (a + shift) % count) for a in range(count)])


def tp_sum(x):
    count = lax.axis_size("tp")
    assert count & (count - 1) == 0
    bit = 1
    while bit < count:
        x = x + lax.ppermute(x, "tp", [(a, a ^ bit) for a in range(count)])
        bit *= 2
    return x


def on_device(
    tokens,
    w_query,
    w_key,
    w_value,
    q_gain,
    k_gain,
    cache_keys,
    cache_values,
    sink_keys,
    sink_values,
    sink_pos,
    cache_len,
    span_len,
    window_len,
):
    req_local, span_local, model_width = tokens.shape
    local_cols = w_query.shape[1]
    seq_count = lax.axis_size("seq")
    seq_index = lax.axis_index("seq")
    token_rows = tokens.reshape(req_local * span_local, model_width)
    offsets = seq_index * span_local + jnp.arange(span_local, dtype=jnp.int32)
    positions = (cache_len[:, None] + offsets[None, :]).reshape(-1)
    wq_all = lax.all_gather(w_query, ("req", "seq"), axis=0, tiled=True)
    wkv_all = lax.all_gather(
        jnp.concatenate([w_key, w_value], axis=1), ("req", "seq"), axis=0, tiled=True
    )
    q_proj = jnp.dot(token_rows, wq_all, preferred_element_type=jnp.float32)
    q_squares = tp_sum(jnp.sum(q_proj * q_proj, axis=1))
    q_local = normalize_rotate(q_proj, q_squares, q_gain, positions, D, HEAD_DIM).reshape(
        req_local, span_local, local_cols
    )
    q_parts = jnp.stack([shifted(q_local, "seq", shift) for shift in range(seq_count)])
    c_sum, c_high, c_total = cache_attention(
        q_parts, cache_keys, cache_values, cache_len, window_len, seq_index
    )
    c_stats = jnp.concatenate([c_high, c_total], axis=-1)
    parts_sum = jnp.stack([shifted(c_sum[s], "seq", -s) for s in range(seq_count)])
    parts_stats = jnp.stack([shifted(c_stats[s], "seq", -s) for s in range(seq_count)])
    wkv_all, parts_sum, parts_stats = lax.optimization_barrier((wkv_all, parts_sum, parts_stats))
    kv_proj = jnp.dot(token_rows, wkv_all, preferred_element_type=jnp.float32)
    k_proj = kv_proj[:, :local_cols]
    k_squares = tp_sum(jnp.sum(k_proj * k_proj, axis=1))
    k_rot = normalize_rotate(k_proj, k_squares, k_gain, positions, D, HEAD_DIM)
    v_new = kv_proj[:, local_cols:].astype(jnp.bfloat16)
    kv_new = jnp.concatenate([k_rot, v_new], axis=1).reshape(req_local, span_local, 2 * local_cols)
    kv_parts = jnp.stack([shifted(kv_new, "seq", shift) for shift in range(seq_count)])
    scalars = (
        cache_len,
        window_len,
        jnp.reshape(seq_index, (1,)).astype(jnp.int32),
        span_len,
        sink_pos.reshape(-1),
    )
    return span_attention(
        q_local, kv_parts, sink_keys, sink_values, parts_sum, parts_stats, scalars
    )


def pair_cache_kernel(
    len_ref, win_ref, seq_ref, first_ref, q_ref, ck_ref, cv_ref, o_ref, m_ref, l_ref, *, scaling
):
    r = pl.program_id(0)
    length_now = len_ref[r] + first_ref[0]
    window_now = win_ref[r]
    seq_index = seq_ref[0]
    rows, slots = q_ref.shape[1], ck_ref.shape[1]
    heads = q_ref.shape[2] // HEAD_DIM
    dims = (((1,), (1,)), ((), ()))
    row = lax.broadcasted_iota(jnp.int32, (rows, slots), 0)
    slot = lax.broadcasted_iota(jnp.int32, (rows, slots), 1) + seq_index * slots
    edge = length_now + row - window_now
    slot_pos = length_now - 1 - ((length_now - 1 - slot) & (WINDOW - 1))
    allowed = (slot_pos >= 0) & (slot_pos > edge)
    bias = jnp.where(allowed, 0.0, lowest)
    for h in range(heads):
        cols = slice(h * HEAD_DIM, (h + 1) * HEAD_DIM)
        scores = (
            lax.dot_general(q_ref[0, :, cols], ck_ref[0, :, cols], dims, preferred_element_type=jnp.float32)
            * scaling
            + bias
        )
        highest = jnp.max(scores, axis=1, keepdims=True)
        weights = jnp.exp(scores - highest)
        some = highest > lowest
        o_ref[0, h] = jnp.where(
            some,
            jnp.dot(weights.astype(jnp.bfloat16), cv_ref[0, :, cols], preferred_element_type=jnp.float32),
            0.0,
        )
        m_ref[0, h] = highest
        l_ref[0, h] = jnp.where(some, jnp.sum(weights, axis=1, keepdims=True), 0.0)


def pair_span_kernel(
    len_ref, win_ref, sink_pos_ref, seq_ref, q_ref, nk_ref, nv_ref, sk_ref, sv_ref, o_ref, m_ref, l_ref, *, scaling
):
    r = pl.program_id(0)
    length_now = len_ref[r]
    window_now = win_ref[r]
    rows = q_ref.shape[1]
    heads = q_ref.shape[2] // HEAD_DIM
    dims = (((1,), (1,)), ((), ()))
    row = lax.broadcasted_iota(jnp.int32, (rows, rows), 0)
    key = lax.broadcasted_iota(jnp.int32, (rows, rows), 1)
    allowed = key <= row
    row_1 = lax.broadcasted_iota(jnp.int32, (rows, 1), 0)
    edge = length_now + row_1 - window_now
    sink_ok = [sink_pos_ref[r, sink] <= edge for sink in range(SINKS)]
    for h in range(heads):
        cols = slice(h * HEAD_DIM, (h + 1) * HEAD_DIM)
        queries = q_ref[0, :, cols]
        scores = (
            lax.dot_general(queries, nk_ref[0, :, cols], dims, preferred_element_type=jnp.float32)
            * scaling
        )
        query_f = queries.astype(jnp.float32)
        sink_scores = []
        for sink in range(SINKS):
            key_f = sk_ref[0, sink : sink + 1, cols].astype(jnp.float32)
            sink_scores.append(jnp.sum(query_f * key_f, axis=1, keepdims=True) * scaling)
        highest = jnp.max(jnp.where(allowed, scores, lowest), axis=1, keepdims=True)
        for part, ok in zip(sink_scores, sink_ok):
            highest = jnp.maximum(highest, jnp.where(ok, part, lowest))
        weights = jnp.where(allowed, jnp.exp(scores - highest), 0.0)
        totals = jnp.sum(weights, axis=1, keepdims=True)
        summed = jnp.dot(
            weights.astype(jnp.bfloat16), nv_ref[0, :, cols], preferred_element_type=jnp.float32
        )
        for sink in range(SINKS):
            sink_w = jnp.where(sink_ok[sink], jnp.exp(sink_scores[sink] - highest), 0.0)
            totals = totals + sink_w
            value_f = sv_ref[0, sink : sink + 1, cols].astype(jnp.float32)
            summed = summed + sink_w.astype(jnp.bfloat16).astype(jnp.float32) * value_f
        o_ref[0, h] = summed
        m_ref[0, h] = highest
        l_ref[0, h] = totals


def merged_cache_kernel(
    len_ref, win_ref, seq_ref, first_ref, owner_ref, qa_ref, qb_ref, ck_ref, cv_ref, ss_ref, sm_ref,
    sl_ref, o_ref, st_ref, *, scaling, normalize
):
    r = pl.program_id(0)
    length_now = len_ref[r] + first_ref[0]
    window_now = win_ref[r]
    seq_index = seq_ref[0]
    rows, slots = qa_ref.shape[1], ck_ref.shape[1]
    heads_half = ss_ref.shape[1]
    heads = 2 * heads_half
    dims = (((1,), (1,)), ((), ()))
    row = lax.broadcasted_iota(jnp.int32, (rows, slots), 0)
    slot = lax.broadcasted_iota(jnp.int32, (rows, slots), 1) + seq_index * slots
    edge = length_now + row - window_now
    cached = len_ref[r]
    slot_pos = cached - 1 - ((cached - 1 - slot) & (WINDOW - 1))
    allowed = (slot_pos >= 0) & (slot_pos > edge)
    bias = jnp.where(allowed, 0.0, lowest)
    for h in range(heads):
        cols = slice(h * HEAD_DIM, (h + 1) * HEAD_DIM)
        j = h % heads_half
        local = slice(j * HEAD_DIM, (j + 1) * HEAD_DIM)
        here = (h // heads_half) == seq_index
        queries = jnp.where(here, qa_ref[0, :, local], qb_ref[0, :, local])
        scores = (
            lax.dot_general(queries, ck_ref[0, :, cols], dims, preferred_element_type=jnp.float32)
            * scaling
            + bias
        )
        highest = jnp.max(scores, axis=1, keepdims=True)
        weights = jnp.exp(scores - highest)
        some = highest > lowest
        summed = jnp.where(
            some,
            jnp.dot(weights.astype(jnp.bfloat16), cv_ref[0, :, cols], preferred_element_type=jnp.float32),
            0.0,
        )
        totals = jnp.where(some, jnp.sum(weights, axis=1, keepdims=True), 0.0)
        span_high = sm_ref[0, j]
        peak = jnp.maximum(highest, span_high)
        f_cache = jnp.exp(highest - peak)
        f_span = jnp.exp(span_high - peak)
        summed = jnp.where(here, summed * f_cache + ss_ref[0, j] * f_span, summed)
        totals = jnp.where(here, totals * f_cache + sl_ref[0, j] * f_span, totals)
        highest = jnp.where(here, peak, highest)
        if normalize:
            summed = summed / jnp.where(totals > 0, totals, 1.0)
        o_ref[0, :, cols] = summed.astype(o_ref.dtype)
        st_ref[0, h, :, 0:1] = highest
        st_ref[0, h, :, 1:2] = totals


def pair_partials(kernel, scalars, q_spec_index, operands, in_specs, req_local, heads, rows):
    grid_spec = pltpu.PrefetchScalarGridSpec(
        num_scalar_prefetch=len(scalars),
        grid=(req_local,),
        in_specs=in_specs,
        out_specs=[
            pl.BlockSpec((1, heads, rows, HEAD_DIM), lambda r, *_: (r, 0, 0, 0)),
            pl.BlockSpec((1, heads, rows, 1), lambda r, *_: (r, 0, 0, 0)),
            pl.BlockSpec((1, heads, rows, 1), lambda r, *_: (r, 0, 0, 0)),
        ],
    )
    shape = (req_local, heads, rows)
    return pl.pallas_call(
        functools.partial(kernel, scaling=HEAD_DIM ** (-0.5)),
        grid_spec=grid_spec,
        out_shape=[
            jax.ShapeDtypeStruct(shape + (HEAD_DIM,), jnp.float32),
            jax.ShapeDtypeStruct(shape + (1,), jnp.float32),
            jax.ShapeDtypeStruct(shape + (1,), jnp.float32),
        ],
    )(*scalars, *operands)


def merge_parts(first, second):
    s1, m1, l1 = first
    s2, m2, l2 = second
    peak = jnp.maximum(m1, m2)
    f1 = jnp.exp(m1 - peak)
    f2 = jnp.exp(m2 - peak)
    return (s1 * f1 + s2 * f2, peak, l1 * f1 + l2 * f2)


def swap_seq(x):
    return lax.ppermute(x, "seq", [(0, 1), (1, 0)])


def on_device_pair(
    tokens,
    w_query,
    w_key,
    w_value,
    q_gain,
    k_gain,
    cache_keys,
    cache_values,
    sink_keys,
    sink_values,
    sink_pos,
    cache_len,
    span_len,
    window_len,
):
    req_local, span_local, model_width = tokens.shape
    local_cols = w_query.shape[1]
    half = local_cols // 2
    heads_local = local_cols // HEAD_DIM
    heads_half = heads_local // 2
    seq_index = lax.axis_index("seq")
    first = seq_index == 0
    span_total = 2 * span_local
    slot_local = cache_keys.shape[1]
    weights = (w_query, w_key, w_value)
    other = jnp.concatenate(
        [jnp.where(first, w[:, half:], w[:, :half]) for w in weights], axis=1
    )
    got = swap_seq(other)
    mine = jnp.concatenate(
        [jnp.where(first, w[:, :half], w[:, half:]) for w in weights], axis=1
    )
    w_all = lax.all_gather(jnp.concatenate([mine, got], 0), "req", axis=0, tiled=True)
    tokens_other = swap_seq(tokens)
    tokens_all = jnp.where(
        first,
        jnp.concatenate([tokens, tokens_other], axis=1),
        jnp.concatenate([tokens_other, tokens], axis=1),
    )
    row_block = w_query.shape[0]
    blocks = tokens_all.reshape(req_local, span_total, model_width // (2 * row_block), 2, row_block)
    tokens_all = jnp.where(first, blocks, blocks[:, :, :, ::-1, :]).reshape(tokens_all.shape)
    token_rows = tokens_all.reshape(req_local * span_total, model_width)
    proj = jnp.dot(token_rows, w_all, preferred_element_type=jnp.float32)
    q_proj = proj[:, :half]
    k_proj = proj[:, half : 2 * half]
    v_proj = proj[:, 2 * half :]
    squares = jnp.stack([jnp.sum(q_proj * q_proj, axis=1), jnp.sum(k_proj * k_proj, axis=1)])
    squares = tp_sum(squares)
    squares = squares + swap_seq(squares)
    offsets = jnp.arange(span_total, dtype=jnp.int32)
    positions = (cache_len[:, None] + offsets[None, :]).reshape(-1)
    q_gain_half = lax.dynamic_slice_in_dim(q_gain, seq_index * half, half)
    k_gain_half = lax.dynamic_slice_in_dim(k_gain, seq_index * half, half)
    q_half = normalize_rotate(q_proj, squares[0], q_gain_half, positions, D, HEAD_DIM).reshape(
        req_local, span_total, half
    )
    k_half = normalize_rotate(k_proj, squares[1], k_gain_half, positions, D, HEAD_DIM).reshape(
        req_local, span_total, half
    )
    v_half = v_proj.astype(jnp.bfloat16).reshape(req_local, span_total, half)
    q_other = swap_seq(q_half)
    q_full = jnp.where(
        first, jnp.concatenate([q_half, q_other], -1), jnp.concatenate([q_other, q_half], -1)
    )
    seq_arr = jnp.reshape(seq_index, (1,)).astype(jnp.int32)
    head_block = lambda r, *_: (r, 0, 0)
    sink_block = lambda r, len_ref, win_ref, pos_ref, seq_ref: (r, 0, seq_ref[0])
    span_part = pair_partials(
        pair_span_kernel,
        (cache_len, window_len, sink_pos, seq_arr),
        None,
        (q_half, k_half, v_half, sink_keys, sink_values),
        [
            pl.BlockSpec((1, span_total, half), head_block),
            pl.BlockSpec((1, span_total, half), head_block),
            pl.BlockSpec((1, span_total, half), head_block),
            pl.BlockSpec((1, SINKS, half), sink_block),
            pl.BlockSpec((1, SINKS, half), sink_block),
        ],
        req_local,
        heads_half,
        span_total,
    )

    def rows_of(x, owner):
        return lax.dynamic_slice_in_dim(x, owner * span_local, span_local, axis=2)

    def cache_rows(owner, normalize):
        first_row = jnp.reshape(owner * span_local, (1,)).astype(jnp.int32)
        q_block = lambda r, len_ref, win_ref, seq_ref, first_ref, owner_ref: (r, owner_ref[0], 0)
        span_block = lambda r, len_ref, win_ref, seq_ref, first_ref, owner_ref: (
            r,
            0,
            owner_ref[0],
            0,
        )
        grid_spec = pltpu.PrefetchScalarGridSpec(
            num_scalar_prefetch=5,
            grid=(req_local,),
            in_specs=[
                pl.BlockSpec((1, span_local, half), q_block),
                pl.BlockSpec((1, span_local, half), q_block),
                pl.BlockSpec((1, slot_local, local_cols), head_block),
                pl.BlockSpec((1, slot_local, local_cols), head_block),
                pl.BlockSpec((1, heads_half, span_local, HEAD_DIM), span_block),
                pl.BlockSpec((1, heads_half, span_local, 1), span_block),
                pl.BlockSpec((1, heads_half, span_local, 1), span_block),
            ],
            out_specs=[
                pl.BlockSpec((1, span_local, local_cols), lambda r, *_: (r, 0, 0)),
                pl.BlockSpec((1, heads_local, span_local, 2), lambda r, *_: (r, 0, 0, 0)),
            ],
        )
        shape = (req_local, heads_local, span_local)
        return pl.pallas_call(
            functools.partial(
                merged_cache_kernel, scaling=HEAD_DIM ** (-0.5), normalize=normalize
            ),
            grid_spec=grid_spec,
            out_shape=[
                jax.ShapeDtypeStruct(
                    (req_local, span_local, local_cols),
                    jnp.bfloat16 if normalize else jnp.float32,
                ),
                jax.ShapeDtypeStruct(shape + (2,), jnp.float32),
            ],
        )(
            cache_len,
            window_len,
            seq_arr,
            first_row,
            jnp.reshape(owner, (1,)).astype(jnp.int32),
            q_half,
            q_other,
            cache_keys,
            cache_values,
            *span_part,
        )

    far_norm, far_stats = cache_rows(1 - seq_index, True)
    got_norm = swap_seq(far_norm)
    got_stats = swap_seq(far_stats)
    own_sum, own_stats = cache_rows(seq_index, False)
    own_high, own_total = own_stats[..., 0], own_stats[..., 1]
    got_high, got_total = got_stats[..., 0], got_stats[..., 1]
    peak = jnp.maximum(own_high, got_high)
    own_factor = jnp.exp(own_high - peak)
    got_factor = jnp.exp(got_high - peak) * got_total
    total = own_total * own_factor + got_factor

    def per_row(x):
        return jnp.transpose(x, (0, 2, 1))[..., None]

    heads_shape = (req_local, span_local, heads_local, HEAD_DIM)
    total_sum = own_sum.reshape(heads_shape) * per_row(own_factor) + got_norm.reshape(
        heads_shape
    ).astype(jnp.float32) * per_row(got_factor)
    own_offsets = seq_index * span_local + jnp.arange(span_local, dtype=jnp.int32)
    live_rows = (own_offsets[None, :] < span_len[:, None])[:, :, None, None]
    safe_total = jnp.where(live_rows, per_row(total), 1.0)
    mixed = jnp.where(live_rows, total_sum / safe_total, 0.0)
    return mixed.reshape(req_local, span_local, local_cols).astype(jnp.bfloat16)


def solution(mesh):
    placed = (
        P("req", "seq", None),
        P(("req", "seq"), "tp"),
        P(("req", "seq"), "tp"),
        P(("req", "seq"), "tp"),
        P("tp"),
        P("tp"),
        P("req", "seq", "tp"),
        P("req", "seq", "tp"),
        P("req", None, "tp"),
        P("req", None, "tp"),
        P("req", None),
        P("req"),
        P("req"),
        P("req"),
    )
    body = on_device_pair if mesh.shape["seq"] == 2 else on_device
    return jax.shard_map(
        body, mesh=mesh, in_specs=placed, out_specs=P("req", "seq", "tp"), check_vma=False
    )
```
